128 devices in a mesh: tsink: 8 (over x, z_lo), mom: 16 (over y, z_hi, core).
Axes of the slice: x: 4, y: 4, z: 4 (z_hi: 2, z_lo: 2; z = z_hi * 2 + z_lo), core: 2. Of those that a mesh axis runs over, the one named last changes fastest.
Arguments:
- perambulators: bfloat16 [8, 4, 1024, 1024], P('tsink'), may hold values from -0.1875 to 0.1875
- elementals: bfloat16 [8, 16, 1024, 1024], P('tsink', 'mom'), may hold values from -6 to 6
- src_times: int32 [4], replicated, may hold values from 0 to 7, as said below
- diagrams: int32 [128, 2], replicated, may hold values from 0 to 15
Outputs:
- meson_blocks: bfloat16 [8, 16, 1024, 1024], P('tsink', 'mom')
- correlators: float32 [128, 8], P('mom', 'tsink')
The draws below stay inside these ranges and needn't reach their ends.
Inputs may be any that keep to these rules, and one draw needn't show every extreme that they name: `src_times`: distinct time slices; the first and the last time slice are always among them.
All inputs are finite; a program needn't handle non-finite values.
Results may differ from the reference program's by a relative error of at most 0.0055.
Values may be sent and summed in bfloat16 or wider, within the bound.
No kernel may reach another device: no remote copies, remote signals or barrier semaphores. Data moves between devices by JAX's collectives and lax.ppermute only.
A program may use at most 192 MiB of HBM per device.

```python
import math
import jax
import jax.numpy as jnp
import numpy as np
from jax import lax

R = 1024
NSRC = 4
NT = 8
MOMS = 16
DIAGS = 128


def draw_src_times(key, part):
    middle = jax.random.permutation(jax.random.fold_in(key, 11), NT - 2) + 1
    picked = jnp.concatenate([jnp.array([0, NT - 1], jnp.int32), middle[:NSRC - 2].astype(jnp.int32)])
    return jax.random.permutation(jax.random.fold_in(key, 12), picked)


def plant(values, stream_key, low, top_value):
    spot = [jax.random.randint(jax.random.fold_in(stream_key, axis), (), 0, length) for axis, length in enumerate(values.shape)]
    widest = values.shape.index(max(values.shape))
    next_to = spot[:widest] + [(spot[widest] + 1) % values.shape[widest]] + spot[widest + 1:]
    return values.at[tuple(spot)].set(low).at[tuple(next_to)].set(top_value)


def steps_of(key, extent, pieces, low, largest):
    def one(position, parts):
        steps = jax.random.uniform(jax.random.fold_in(jax.random.fold_in(key, 6), position), (parts,), jnp.float32, low / len(pieces), largest / len(pieces))
        return jnp.repeat(jnp.exp(steps), extent[position] // parts).reshape((-1,) + (1,) * (len(extent) - position - 1))

    loudness = one(*pieces[0])
    for cut in pieces[1:]:
        loudness = loudness * one(*cut)
    return loudness


def rank_table(count, lean):
    portions = [(1 << 20) // math.isqrt(rank ** lean) + 1 for rank in range(1, count + 1)]
    scale = 1 + sum(portions) // (1 << 30)
    return np.cumsum(np.array([max(1, weight // scale) for weight in portions]))


def ranked(key, shape, number_of, lean):
    table = rank_table(number_of, lean)
    lot = jax.random.randint(jax.random.fold_in(key, 1), shape, 0, int(table[number_of - 1]))
    rank = jnp.searchsorted(jnp.asarray(table, jnp.int32), lot, side="right")
    return jax.random.permutation(jax.random.fold_in(key, 2), number_of)[rank].astype(jnp.int32)


def scatter_about(own_key, extent, scale, bound, pieces=(), held_as=jnp.bfloat16):
    entries = jax.random.normal(own_key, extent, jnp.float32) * scale
    if len(pieces) > 0:
        entries = steps_of(own_key, extent, pieces, -0.22, 0.18) * entries
    return jnp.clip(entries, min=-bound, max=bound).astype(held_as)


def setup_inputs(seed: int = 0) -> dict:
    keys = jax.random.split(jax.random.key(seed), 5)
    return {
        "perambulators": scatter_about(keys[0], (NT, NSRC, R, R), R ** -0.5, 0.1875, ((0, 8),)),
        "elementals": scatter_about(keys[1], (NT, MOMS, R, R), 1.0, 6.0, ((0, 8), (1, 16))),
        "src_times": draw_src_times(jax.random.fold_in(keys[4], 71), 0),
        "diagrams": plant(ranked(keys[3], (DIAGS, 2), MOMS, 2), jax.random.fold_in(keys[3], 3), 0, MOMS - 1).astype(jnp.int32),
    }


def meson_block(propagators, chosen):
    summed = jnp.zeros((R, R), jnp.float32)
    for source in range(NSRC):
        half_product = lax.dot_general(chosen[source], propagators[source], (((1,), (1,)), ((), ())), preferred_element_type=jnp.float32).astype(jnp.bfloat16)
        summed = summed + jnp.dot(propagators[source], half_product, preferred_element_type=jnp.float32)
    return summed.astype(jnp.bfloat16)


def reference(perambulators, elementals, src_times, diagrams):
    chosen_all = elementals[src_times.astype(jnp.int32)]

    def per_sink(sink):
        propagators = perambulators[sink]

        def per_momentum(moment):
            return meson_block(propagators, chosen_all[:, moment])

        return lax.map(per_momentum, jnp.arange(MOMS, dtype=jnp.int32))

    blocks_all = lax.map(per_sink, jnp.arange(NT, dtype=jnp.int32))

    def per_diagram(diagram_pair):
        first = blocks_all[:, diagram_pair[0]].astype(jnp.float32)
        second = blocks_all[:, diagram_pair[1]].astype(jnp.float32)
        return jnp.einsum("tij,tji->t", first, second) / R

    correlators = lax.map(per_diagram, diagrams)
    return blocks_all, correlators
```

```python
import jax
import jax.numpy as jnp
from jax import lax
from jax.sharding import PartitionSpec as P

NSRC = 4


def source_elementals(own_elemental, src_times):
    n_t = lax.axis_size("tsink")
    order = own_elemental.shape[0]
    pieces = own_elemental.reshape(n_t, order // n_t, order)
    received = lax.all_to_all(pieces, "tsink", 0, 0)
    chosen = received[src_times]
    elementals = []
    for source in range(NSRC):
        gathered = lax.all_gather(chosen[source], "tsink", axis=0, tiled=True)
        elementals.append(gathered)
    return elementals


def body(perambulators, elementals, src_times, diagrams):
    propagators = perambulators[0]
    own_elemental = elementals[0, 0]
    block_order = propagators.shape[1]
    chosen = source_elementals(own_elemental, src_times)
    summed = jnp.zeros((block_order, block_order), jnp.float32)
    for source in range(NSRC):
        half_product = lax.dot_general(
            chosen[source],
            propagators[source],
            (((1,), (1,)), ((), ())),
            preferred_element_type=jnp.float32,
        ).astype(jnp.bfloat16)
        summed = summed + jnp.dot(
            propagators[source], half_product, preferred_element_type=jnp.float32
        )
    meson = summed.astype(jnp.bfloat16)

    n_m = lax.axis_size("mom")
    rows = block_order // n_m
    slices = jnp.stack(
        [meson.reshape(n_m, rows, block_order), meson.T.reshape(n_m, rows, block_order)],
        axis=1,
    )
    received = lax.all_to_all(slices, "mom", 0, 0)
    own_rows = received[:, 0].reshape(n_m, rows * block_order)
    own_cols = received[:, 1].reshape(n_m, rows * block_order)
    partial = lax.dot_general(
        own_rows, own_cols, (((1,), (1,)), ((), ())), preferred_element_type=jnp.float32
    )
    pair_traces = lax.psum(partial, "mom") / block_order

    per_device = diagrams.shape[0] // n_m
    own_diagrams = lax.dynamic_slice_in_dim(
        diagrams, lax.axis_index("mom") * per_device, per_device, 0
    )
    traces = pair_traces[own_diagrams[:, 0], own_diagrams[:, 1]]
    correlators = traces[:, None]
    return (meson[None, None], correlators)


def solution(mesh):
    in_specs = (P("tsink", None, None, None), P("tsink", "mom", None, None), P(), P())
    out_specs = (P("tsink", "mom", None, None), P("mom", "tsink"))
    return jax.shard_map(body, mesh=mesh, in_specs=in_specs, out_specs=out_specs, check_vma=False)
```

```python
import jax
import jax.numpy as jnp
from jax import lax
from jax.sharding import PartitionSpec as P

NSRC = 4


def source_elementals(own_elemental, src_times):
    n_t = lax.axis_size("tsink")
    order = own_elemental.shape[0]
    pieces = own_elemental.reshape(n_t, order // n_t, order)
    received = lax.all_to_all(pieces, "tsink", 0, 0)
    chosen = received[src_times]
    gathered = lax.all_gather(chosen, "tsink", axis=1, tiled=True)
    return [gathered[source] for source in range(NSRC)]


def body(perambulators, elementals, src_times, diagrams):
    propagators = perambulators[0]
    own_elemental = elementals[0, 0]
    block_order = propagators.shape[1]
    chosen = source_elementals(own_elemental, src_times)
    summed = jnp.zeros((block_order, block_order), jnp.float32)
    for source in range(NSRC):
        half_product = lax.dot_general(
            chosen[source],
            propagators[source],
            (((1,), (1,)), ((), ())),
            preferred_element_type=jnp.float32,
        ).astype(jnp.bfloat16)
        summed = summed + jnp.dot(
            propagators[source], half_product, preferred_element_type=jnp.float32
        )
    meson = summed.astype(jnp.bfloat16)

    n_m = lax.axis_size("mom")
    rows = block_order // n_m
    slices = jnp.stack(
        [meson.reshape(n_m, rows, block_order), meson.T.reshape(n_m, rows, block_order)],
        axis=1,
    )
    received = lax.all_to_all(slices, "mom", 0, 0)
    own_rows = received[:, 0].reshape(n_m, rows * block_order)
    own_cols = received[:, 1].reshape(n_m, rows * block_order)
    partial = lax.dot_general(
        own_rows, own_cols, (((1,), (1,)), ((), ())), preferred_element_type=jnp.float32
    )
    per_diagram = partial[diagrams[:, 0], diagrams[:, 1]]
    spread = lax.all_to_all(per_diagram.reshape(n_m, -1), "mom", 0, 0)
    correlators = (jnp.sum(spread, axis=0) / block_order)[:, None]
    return (meson[None, None], correlators)


def solution(mesh):
    in_specs = (P("tsink", None, None, None), P("tsink", "mom", None, None), P(), P())
    out_specs = (P("tsink", "mom", None, None), P("mom", "tsink"))
    return jax.shard_map(body, mesh=mesh, in_specs=in_specs, out_specs=out_specs, check_vma=False)
```

```python
import jax
import jax.numpy as jnp
from jax import lax
from jax.sharding import PartitionSpec as P

NSRC = 4


def shifted(block, offset, n_t):
    pairs = [(t, (t + offset) % n_t) for t in range(n_t)]
    return lax.ppermute(block, "tsink", pairs)


def swapped(block, n_t):
    return lax.ppermute(block, "tsink", [(t, t ^ 1) for t in range(n_t)])


def source_pieces(own_elemental, src_times):
    n_t = lax.axis_size("tsink")
    order = own_elemental.shape[0]
    rows = order // n_t
    half = rows // 2
    pieces = own_elemental.reshape(n_t, rows, order)
    received = lax.all_to_all(pieces, "tsink", 0, 0)
    own = received[src_times]
    t = lax.axis_index("tsink")
    step = 2
    partner = swapped(own, n_t)
    from_left = shifted(own, step, n_t)
    from_right = shifted(own, -step, n_t)
    far = jnp.concatenate(
        [shifted(from_left[:, :half], step, n_t), shifted(from_right[:, half:], -step, n_t)], axis=1
    )
    partner_left = shifted(partner, step, n_t)
    partner_right = shifted(partner, -step, n_t)
    partner_far = jnp.concatenate(
        [shifted(partner_left[:, :half], step, n_t), shifted(partner_right[:, half:], -step, n_t)],
        axis=1,
    )
    return [
        (t, own),
        (t ^ 1, partner),
        ((t - step) % n_t, from_left),
        ((t + step) % n_t, from_right),
        ((t + 2 * step) % n_t, far),
        ((t - step) % n_t ^ 1, partner_left),
        ((t + step) % n_t ^ 1, partner_right),
        ((t + 2 * step) % n_t ^ 1, partner_far),
    ]


def body(perambulators, elementals, src_times, diagrams):
    propagators = perambulators[0]
    own_elemental = elementals[0, 0]
    block_order = propagators.shape[1]
    pieces = source_pieces(own_elemental, src_times)
    rows = pieces[0][1].shape[1]
    halves = jnp.zeros((NSRC, block_order, block_order), jnp.bfloat16)
    for origin, piece in pieces:
        block = jnp.einsum(
            "sik,sjk->sij", piece, propagators, preferred_element_type=jnp.float32
        ).astype(jnp.bfloat16)
        halves = lax.dynamic_update_slice_in_dim(halves, block, origin * rows, 1)
    summed = jnp.zeros((block_order, block_order), jnp.float32)
    for source in range(NSRC):
        summed = summed + jnp.dot(
            propagators[source], halves[source], preferred_element_type=jnp.float32
        )
    meson = summed.astype(jnp.bfloat16)

    n_m = lax.axis_size("mom")
    rows = block_order // n_m
    slices = jnp.stack(
        [meson.reshape(n_m, rows, block_order), meson.T.reshape(n_m, rows, block_order)],
        axis=1,
    )
    received = lax.all_to_all(slices, "mom", 0, 0)
    own_rows = received[:, 0].reshape(n_m, rows * block_order)
    own_cols = received[:, 1].reshape(n_m, rows * block_order)
    partial = lax.dot_general(
        own_rows, own_cols, (((1,), (1,)), ((), ())), preferred_element_type=jnp.float32
    )
    per_diagram = partial[diagrams[:, 0], diagrams[:, 1]]
    spread = lax.all_to_all(per_diagram.reshape(n_m, -1), "mom", 0, 0)
    correlators = (jnp.sum(spread, axis=0) / block_order)[:, None]
    return (meson[None, None], correlators)


def solution(mesh):
    in_specs = (P("tsink", None, None, None), P("tsink", "mom", None, None), P(), P())
    out_specs = (P("tsink", "mom", None, None), P("mom", "tsink"))
    return jax.shard_map(body, mesh=mesh, in_specs=in_specs, out_specs=out_specs, check_vma=False)
```

```python
import jax
import jax.numpy as jnp
from jax import lax
from jax.sharding import PartitionSpec as P

NSRC = 4


def shifted(block, offset, n_t):
    pairs = [(t, (t + offset) % n_t) for t in range(n_t)]
    return lax.ppermute(block, "tsink", pairs)


def swapped(block, n_t):
    return lax.ppermute(block, "tsink", [(t, t ^ 1) for t in range(n_t)])


def source_pieces(own_elemental, src_times):
    n_t = lax.axis_size("tsink")
    order = own_elemental.shape[0]
    rows = order // n_t
    half = rows // 2
    pieces = own_elemental.reshape(n_t, rows, order)
    received = lax.all_to_all(pieces, "tsink", 0, 0)
    own = received[src_times]
    t = lax.axis_index("tsink")
    step = 2
    partner = swapped(own, n_t)
    from_left = shifted(own, step, n_t)
    from_right = shifted(own, -step, n_t)
    far = jnp.concatenate(
        [shifted(from_left[:, :half], step, n_t), shifted(from_right[:, half:], -step, n_t)], axis=1
    )
    partner_left = shifted(partner, step, n_t)
    partner_right = shifted(partner, -step, n_t)
    partner_far = jnp.concatenate(
        [shifted(partner_left[:, :half], step, n_t), shifted(partner_right[:, half:], -step, n_t)],
        axis=1,
    )
    return [
        (t, own),
        (t ^ 1, partner),
        ((t - step) % n_t, from_left),
        ((t + step) % n_t, from_right),
        ((t + 2 * step) % n_t, far),
        ((t - step) % n_t ^ 1, partner_left),
        ((t + step) % n_t ^ 1, partner_right),
        ((t + 2 * step) % n_t ^ 1, partner_far),
    ]


def body(perambulators, elementals, src_times, diagrams):
    propagators = perambulators[0]
    own_elemental = elementals[0, 0]
    block_order = propagators.shape[1]
    pieces = source_pieces(own_elemental, src_times)
    rows = pieces[0][1].shape[1]
    halves = jnp.zeros((NSRC, block_order, block_order), jnp.bfloat16)
    for origin, piece in pieces:
        block = jnp.einsum(
            "sik,sjk->sij", piece, propagators, preferred_element_type=jnp.float32
        ).astype(jnp.bfloat16)
        halves = lax.dynamic_update_slice_in_dim(halves, block, origin * rows, 1)
    summed = jnp.zeros((block_order, block_order), jnp.float32)
    for source in range(NSRC):
        summed = summed + jnp.dot(
            propagators[source], halves[source], preferred_element_type=jnp.float32
        )
    meson = summed.astype(jnp.bfloat16)

    n_m = lax.axis_size("mom")
    width = 128
    upper, upper_t, weights = [], [], []
    transposed = meson.T
    for col in range(block_order // width):
        height = width * (col + 1)
        upper.append(meson[:height, col * width:(col + 1) * width])
        upper_t.append(transposed[:height, col * width:(col + 1) * width])
        row_index = lax.broadcasted_iota(jnp.int32, (height, width), 0)
        col_index = lax.broadcasted_iota(jnp.int32, (height, width), 1) + col * width
        weights.append(
            jnp.where(row_index < col_index, 1.0, jnp.where(row_index == col_index, 0.5, 0.0))
        )
    weight = jnp.concatenate(weights, axis=0).astype(jnp.bfloat16)
    upper = jnp.concatenate(upper, axis=0) * weight
    upper_t = jnp.concatenate(upper_t, axis=0)
    share = upper.shape[0] // n_m
    slices = jnp.stack(
        [upper.reshape(n_m, share, width), upper_t.reshape(n_m, share, width)], axis=1
    )
    received = lax.all_to_all(slices, "mom", 0, 0)
    own_rows = received[:, 0].reshape(n_m, share * width)
    own_cols = received[:, 1].reshape(n_m, share * width)
    partial = lax.dot_general(
        own_rows, own_cols, (((1,), (1,)), ((), ())), preferred_element_type=jnp.float32
    )
    partial = partial + partial.T
    per_diagram = partial[diagrams[:, 0], diagrams[:, 1]]
    spread = lax.all_to_all(per_diagram.reshape(n_m, -1), "mom", 0, 0)
    correlators = (jnp.sum(spread, axis=0) / block_order)[:, None]
    return (meson[None, None], correlators)


def solution(mesh):
    in_specs = (P("tsink", None, None, None), P("tsink", "mom", None, None), P(), P())
    out_specs = (P("tsink", "mom", None, None), P("mom", "tsink"))
    return jax.shard_map(body, mesh=mesh, in_specs=in_specs, out_specs=out_specs, check_vma=False)
```

```python
import jax
import jax.numpy as jnp
from jax import lax
from jax.sharding import PartitionSpec as P

NSRC = 4


def shifted(block, offset, n_t):
    pairs = [(t, (t + offset) % n_t) for t in range(n_t)]
    return lax.ppermute(block, "tsink", pairs)


def swapped(block, n_t):
    return lax.ppermute(block, "tsink", [(t, t ^ 1) for t in range(n_t)])


def source_pieces(own_elemental, src_times):
    n_t = lax.axis_size("tsink")
    order = own_elemental.shape[0]
    rows = order // n_t
    half = rows // 2
    pieces = own_elemental.reshape(n_t, rows, order)
    received = lax.all_to_all(pieces, "tsink", 0, 0)
    own = received[src_times]
    t = lax.axis_index("tsink")
    step = 2
    partner = swapped(own, n_t)
    from_left = shifted(own, step, n_t)
    from_right = shifted(own, -step, n_t)
    far = jnp.concatenate(
        [shifted(from_left[:, :half], step, n_t), shifted(from_right[:, half:], -step, n_t)], axis=1
    )
    partner_left = shifted(partner, step, n_t)
    partner_right = shifted(partner, -step, n_t)
    partner_far = jnp.concatenate(
        [shifted(partner_left[:, :half], step, n_t), shifted(partner_right[:, half:], -step, n_t)],
        axis=1,
    )
    return [
        (t, own),
        (t ^ 1, partner),
        ((t - step) % n_t, from_left),
        ((t + step) % n_t, from_right),
        ((t + 2 * step) % n_t, far),
        ((t - step) % n_t ^ 1, partner_left),
        ((t + step) % n_t ^ 1, partner_right),
        ((t + 2 * step) % n_t ^ 1, partner_far),
    ]


def body(perambulators, elementals, src_times, diagrams):
    propagators = perambulators[0]
    own_elemental = elementals[0, 0]
    block_order = propagators.shape[1]
    pieces = source_pieces(own_elemental, src_times)
    rows = pieces[0][1].shape[1]
    summed = jnp.zeros((block_order, block_order), jnp.float32)
    for origin, piece in pieces:
        half_product = jnp.einsum(
            "sik,sjk->sij", piece, propagators, preferred_element_type=jnp.float32
        ).astype(jnp.bfloat16)
        columns = lax.dynamic_slice_in_dim(propagators, origin * rows, rows, 2)
        summed = summed + jnp.einsum(
            "sik,skj->ij", columns, half_product, preferred_element_type=jnp.float32
        )
    meson = summed.astype(jnp.bfloat16)

    n_m = lax.axis_size("mom")
    width = 128
    upper, upper_t, weights = [], [], []
    transposed = meson.T
    for col in range(block_order // width):
        height = width * (col + 1)
        upper.append(meson[:height, col * width:(col + 1) * width])
        upper_t.append(transposed[:height, col * width:(col + 1) * width])
        row_index = lax.broadcasted_iota(jnp.int32, (height, width), 0)
        col_index = lax.broadcasted_iota(jnp.int32, (height, width), 1) + col * width
        weights.append(
            jnp.where(row_index < col_index, 1.0, jnp.where(row_index == col_index, 0.5, 0.0))
        )
    weight = jnp.concatenate(weights, axis=0).astype(jnp.bfloat16)
    upper = jnp.concatenate(upper, axis=0) * weight
    upper_t = jnp.concatenate(upper_t, axis=0)
    share = upper.shape[0] // n_m
    slices = jnp.stack(
        [upper.reshape(n_m, share, width), upper_t.reshape(n_m, share, width)], axis=1
    )
    received = lax.all_to_all(slices, "mom", 0, 0)
    own_rows = received[:, 0].reshape(n_m, share * width)
    own_cols = received[:, 1].reshape(n_m, share * width)
    partial = lax.dot_general(
        own_rows, own_cols, (((1,), (1,)), ((), ())), preferred_element_type=jnp.float32
    )
    partial = partial + partial.T
    per_diagram = partial[diagrams[:, 0], diagrams[:, 1]]
    spread = lax.all_to_all(per_diagram.reshape(n_m, -1), "mom", 0, 0)
    correlators = (jnp.sum(spread, axis=0) / block_order)[:, None]
    return (meson[None, None], correlators)


def solution(mesh):
    in_specs = (P("tsink", None, None, None), P("tsink", "mom", None, None), P(), P())
    out_specs = (P("tsink", "mom", None, None), P("mom", "tsink"))
    return jax.shard_map(body, mesh=mesh, in_specs=in_specs, out_specs=out_specs, check_vma=False)
```

```python
import jax
import jax.numpy as jnp
from jax import lax
from jax.sharding import PartitionSpec as P

NSRC = 4


def shifted(block, offset, n_t):
    pairs = [(t, (t + offset) % n_t) for t in range(n_t)]
    return lax.ppermute(block, "tsink", pairs)


def swapped(block, n_t):
    return lax.ppermute(block, "tsink", [(t, t ^ 1) for t in range(n_t)])


def source_pieces(own_elemental, src_times):
    n_t = lax.axis_size("tsink")
    order = own_elemental.shape[0]
    rows = order // n_t
    half = rows // 2
    quarter = half // 2
    pieces = own_elemental.reshape(n_t, rows, order)
    received = lax.all_to_all(pieces, "tsink", 0, 0)
    own = received[src_times]
    t = lax.axis_index("tsink")
    step = 2
    from_left = shifted(own, step, n_t)
    from_right = shifted(own, -step, n_t)
    partner_a = swapped(own[:, :half], n_t)
    far = jnp.concatenate(
        [shifted(from_left[:, :half], step, n_t), shifted(from_right[:, half:], -step, n_t)], axis=1
    )
    partner_b = swapped(
        jnp.stack([own[:, half:], from_left[:, half:], from_right[:, half:]]), n_t
    )
    partner_left_a = shifted(partner_a, step, n_t)
    partner_right_a = shifted(partner_a, -step, n_t)
    partner_far_a = jnp.concatenate(
        [
            shifted(partner_left_a[:, :quarter], step, n_t),
            shifted(partner_right_a[:, quarter:], -step, n_t),
        ],
        axis=1,
    )
    partner_far_b = swapped(far[:, half:], n_t)
    return [
        (t, own),
        ((t - step) % n_t, from_left),
        ((t + step) % n_t, from_right),
        ((t + 2 * step) % n_t, far),
        (t ^ 1, jnp.concatenate([partner_a, partner_b[0]], axis=1)),
        ((t - step) % n_t ^ 1, jnp.concatenate([partner_left_a, partner_b[1]], axis=1)),
        ((t + step) % n_t ^ 1, jnp.concatenate([partner_right_a, partner_b[2]], axis=1)),
        ((t + 2 * step) % n_t ^ 1, jnp.concatenate([partner_far_a, partner_far_b], axis=1)),
    ]


def body(perambulators, elementals, src_times, diagrams):
    propagators = perambulators[0]
    own_elemental = elementals[0, 0]
    block_order = propagators.shape[1]
    pieces = source_pieces(own_elemental, src_times)
    rows = pieces[0][1].shape[1]
    halves = jnp.zeros((NSRC, block_order, block_order), jnp.bfloat16)
    for origin, piece in pieces:
        block = jnp.einsum(
            "sik,sjk->sij", piece, propagators, preferred_element_type=jnp.float32
        ).astype(jnp.bfloat16)
        halves = lax.dynamic_update_slice_in_dim(halves, block, origin * rows, 1)
    summed = jnp.zeros((block_order, block_order), jnp.float32)
    for source in range(NSRC):
        summed = summed + jnp.dot(
            propagators[source], halves[source], preferred_element_type=jnp.float32
        )
    meson = summed.astype(jnp.bfloat16)

    n_m = lax.axis_size("mom")
    width = 128
    upper, upper_t, weights = [], [], []
    transposed = meson.T
    for col in range(block_order // width):
        height = width * (col + 1)
        upper.append(meson[:height, col * width:(col + 1) * width])
        upper_t.append(transposed[:height, col * width:(col + 1) * width])
        row_index = lax.broadcasted_iota(jnp.int32, (height, width), 0)
        col_index = lax.broadcasted_iota(jnp.int32, (height, width), 1) + col * width
        weights.append(
            jnp.where(row_index < col_index, 1.0, jnp.where(row_index == col_index, 0.5, 0.0))
        )
    weight = jnp.concatenate(weights, axis=0).astype(jnp.bfloat16)
    upper = jnp.concatenate(upper, axis=0) * weight
    upper_t = jnp.concatenate(upper_t, axis=0)
    share = upper.shape[0] // n_m
    slices = jnp.stack(
        [upper.reshape(n_m, share, width), upper_t.reshape(n_m, share, width)], axis=1
    )
    received = lax.all_to_all(slices, "mom", 0, 0)
    own_rows = received[:, 0].reshape(n_m, share * width)
    own_cols = received[:, 1].reshape(n_m, share * width)
    partial = lax.dot_general(
        own_rows, own_cols, (((1,), (1,)), ((), ())), preferred_element_type=jnp.float32
    )
    partial = partial + partial.T
    per_diagram = partial[diagrams[:, 0], diagrams[:, 1]]
    spread = lax.all_to_all(per_diagram.reshape(n_m, -1), "mom", 0, 0)
    correlators = (jnp.sum(spread, axis=0) / block_order)[:, None]
    return (meson[None, None], correlators)


def solution(mesh):
    in_specs = (P("tsink", None, None, None), P("tsink", "mom", None, None), P(), P())
    out_specs = (P("tsink", "mom", None, None), P("mom", "tsink"))
    return jax.shard_map(body, mesh=mesh, in_specs=in_specs, out_specs=out_specs, check_vma=False)
```

```python
import jax
import jax.numpy as jnp
from jax import lax
from jax.sharding import PartitionSpec as P

NSRC = 4


def shifted(block, offset, n_t):
    pairs = [(t, (t + offset) % n_t) for t in range(n_t)]
    return lax.ppermute(block, "tsink", pairs)


def swapped(block, n_t):
    return lax.ppermute(block, "tsink", [(t, t ^ 1) for t in range(n_t)])


def source_pieces(own_elemental, src_times):
    n_t = lax.axis_size("tsink")
    order = own_elemental.shape[0]
    rows = order // n_t
    half = rows // 2
    quarter = half // 2
    pieces = own_elemental.reshape(n_t, rows, order)
    received = lax.all_to_all(pieces, "tsink", 0, 0)
    own = received[src_times]
    t = lax.axis_index("tsink")
    step = 2
    from_left = shifted(own, step, n_t)
    from_right = shifted(own, -step, n_t)
    partner_a = swapped(own[:, :half], n_t)
    far = jnp.concatenate(
        [shifted(from_left[:, :half], step, n_t), shifted(from_right[:, half:], -step, n_t)], axis=1
    )
    partner_b = swapped(
        jnp.stack([own[:, half:], from_left[:, half:], from_right[:, half:]]), n_t
    )
    partner_left_a = shifted(partner_a, step, n_t)
    partner_right_a = shifted(partner_a, -step, n_t)
    partner_far_a = jnp.concatenate(
        [
            shifted(partner_left_a[:, :quarter], step, n_t),
            shifted(partner_right_a[:, quarter:], -step, n_t),
        ],
        axis=1,
    )
    partner_far_b = swapped(far[:, half:], n_t)
    return [
        (t, own),
        ((t - step) % n_t, from_left),
        ((t + step) % n_t, from_right),
        ((t + 2 * step) % n_t, far),
        (t ^ 1, jnp.concatenate([partner_a, partner_b[0]], axis=1)),
        ((t - step) % n_t ^ 1, jnp.concatenate([partner_left_a, partner_b[1]], axis=1)),
        ((t + step) % n_t ^ 1, jnp.concatenate([partner_right_a, partner_b[2]], axis=1)),
        ((t + 2 * step) % n_t ^ 1, jnp.concatenate([partner_far_a, partner_far_b], axis=1)),
    ]


def body(perambulators, elementals, src_times, diagrams):
    propagators = perambulators[0]
    own_elemental = elementals[0, 0]
    block_order = propagators.shape[1]
    pieces = source_pieces(own_elemental, src_times)
    rows = pieces[0][1].shape[1]
    columns = jnp.concatenate(
        [lax.dynamic_slice_in_dim(propagators, origin * rows, rows, 2) for origin, _ in pieces],
        axis=2,
    )
    blocks = [
        jnp.einsum(
            "sik,sjk->sij", piece, propagators, preferred_element_type=jnp.float32
        ).astype(jnp.bfloat16)
        for _, piece in pieces
    ]
    halves = jnp.concatenate(blocks, axis=1)
    early = 4 * rows
    summed = jnp.zeros((block_order, block_order), jnp.float32)
    for source in range(NSRC):
        summed = summed + jnp.dot(
            columns[source, :, :early], halves[source, :early], preferred_element_type=jnp.float32
        )
    for source in range(NSRC):
        summed = summed + jnp.dot(
            columns[source, :, early:], halves[source, early:], preferred_element_type=jnp.float32
        )
    meson = summed.astype(jnp.bfloat16)

    n_m = lax.axis_size("mom")
    width = 128
    upper, upper_t, weights = [], [], []
    transposed = meson.T
    for col in range(block_order // width):
        height = width * (col + 1)
        upper.append(meson[:height, col * width:(col + 1) * width])
        upper_t.append(transposed[:height, col * width:(col + 1) * width])
        row_index = lax.broadcasted_iota(jnp.int32, (height, width), 0)
        col_index = lax.broadcasted_iota(jnp.int32, (height, width), 1) + col * width
        weights.append(
            jnp.where(row_index < col_index, 1.0, jnp.where(row_index == col_index, 0.5, 0.0))
        )
    weight = jnp.concatenate(weights, axis=0).astype(jnp.bfloat16)
    upper = jnp.concatenate(upper, axis=0) * weight
    upper_t = jnp.concatenate(upper_t, axis=0)
    share = upper.shape[0] // n_m
    slices = jnp.stack(
        [upper.reshape(n_m, share, width), upper_t.reshape(n_m, share, width)], axis=1
    )
    received = lax.all_to_all(slices, "mom", 0, 0)
    own_rows = received[:, 0].reshape(n_m, share * width)
    own_cols = received[:, 1].reshape(n_m, share * width)
    partial = lax.dot_general(
        own_rows, own_cols, (((1,), (1,)), ((), ())), preferred_element_type=jnp.float32
    )
    partial = partial + partial.T
    per_diagram = partial[diagrams[:, 0], diagrams[:, 1]]
    spread = lax.all_to_all(per_diagram.reshape(n_m, -1), "mom", 0, 0)
    correlators = (jnp.sum(spread, axis=0) / block_order)[:, None]
    return (meson[None, None], correlators)


def solution(mesh):
    in_specs = (P("tsink", None, None, None), P("tsink", "mom", None, None), P(), P())
    out_specs = (P("tsink", "mom", None, None), P("mom", "tsink"))
    return jax.shard_map(body, mesh=mesh, in_specs=in_specs, out_specs=out_specs, check_vma=False)
```

```python
import jax
import jax.numpy as jnp
from jax import lax
from jax.sharding import PartitionSpec as P

NSRC = 4


def shifted(block, offset, n_t):
    pairs = [(t, (t + offset) % n_t) for t in range(n_t)]
    return lax.ppermute(block, "tsink", pairs)


def swapped(block, n_t):
    return lax.ppermute(block, "tsink", [(t, t ^ 1) for t in range(n_t)])


def source_pieces(own_elemental, src_times):
    n_t = lax.axis_size("tsink")
    order = own_elemental.shape[0]
    rows = order // n_t
    half = rows // 2
    pieces = own_elemental.reshape(n_t, rows, order)
    received = lax.all_to_all(pieces, "tsink", 0, 0)
    own = received[src_times]
    t = lax.axis_index("tsink")
    step = 2
    partner = swapped(own, n_t)
    from_left = shifted(own, step, n_t)
    from_right = shifted(own, -step, n_t)
    far = jnp.concatenate(
        [shifted(from_left[:, :half], step, n_t), shifted(from_right[:, half:], -step, n_t)], axis=1
    )
    partner_left = shifted(partner, step, n_t)
    partner_right = shifted(partner, -step, n_t)
    partner_far = jnp.concatenate(
        [shifted(partner_left[:, :half], step, n_t), shifted(partner_right[:, half:], -step, n_t)],
        axis=1,
    )
    return [
        (t, own),
        (t ^ 1, partner),
        ((t - step) % n_t, from_left),
        ((t + step) % n_t, from_right),
        ((t + 2 * step) % n_t, far),
        ((t - step) % n_t ^ 1, partner_left),
        ((t + step) % n_t ^ 1, partner_right),
        ((t + 2 * step) % n_t ^ 1, partner_far),
    ]


def body(perambulators, elementals, src_times, diagrams):
    propagators = perambulators[0]
    own_elemental = elementals[0, 0]
    block_order = propagators.shape[1]
    pieces = source_pieces(own_elemental, src_times)
    rows = pieces[0][1].shape[1]
    halves = jnp.zeros((NSRC, block_order, block_order), jnp.bfloat16)
    for origin, piece in pieces:
        block = jnp.einsum(
            "sik,sjk->sij", piece, propagators, preferred_element_type=jnp.float32
        ).astype(jnp.bfloat16)
        halves = lax.dynamic_update_slice_in_dim(halves, block, origin * rows, 1)
    summed = jnp.zeros((block_order, block_order), jnp.float32)
    for source in range(NSRC):
        summed = summed + jnp.dot(
            propagators[source], halves[source], preferred_element_type=jnp.float32
        )
    meson = summed.astype(jnp.bfloat16)

    n_m = lax.axis_size("mom")
    width = 128
    upper, upper_t, weights = [], [], []
    transposed = meson.T
    for col in range(block_order // width):
        height = width * (col + 1)
        upper.append(meson[:height, col * width:(col + 1) * width])
        upper_t.append(transposed[:height, col * width:(col + 1) * width])
        row_index = lax.broadcasted_iota(jnp.int32, (height, width), 0)
        col_index = lax.broadcasted_iota(jnp.int32, (height, width), 1) + col * width
        weights.append(
            jnp.where(row_index < col_index, 1.0, jnp.where(row_index == col_index, 0.5, 0.0))
        )
    weight = jnp.concatenate(weights, axis=0).astype(jnp.bfloat16)
    upper = jnp.concatenate(upper, axis=0) * weight
    upper_t = jnp.concatenate(upper_t, axis=0)
    share = upper.shape[0] // n_m
    slices = jnp.concatenate(
        [upper.reshape(n_m, share, width), upper_t.reshape(n_m, share, width)], axis=1
    )
    received = lax.all_to_all(slices, "mom", 0, 0)
    own_rows = received[:, :share].reshape(n_m, share * width)
    own_cols = received[:, share:].reshape(n_m, share * width)
    partial = lax.dot_general(
        own_rows, own_cols, (((1,), (1,)), ((), ())), preferred_element_type=jnp.float32
    )
    partial = partial + partial.T
    per_diagram = partial[diagrams[:, 0], diagrams[:, 1]]
    spread = lax.all_to_all(per_diagram.reshape(n_m, -1), "mom", 0, 0)
    correlators = (jnp.sum(spread, axis=0) / block_order)[:, None]
    return (meson[None, None], correlators)


def solution(mesh):
    in_specs = (P("tsink", None, None, None), P("tsink", "mom", None, None), P(), P())
    out_specs = (P("tsink", "mom", None, None), P("mom", "tsink"))
    return jax.shard_map(body, mesh=mesh, in_specs=in_specs, out_specs=out_specs, check_vma=False)
```

```python
import numpy as np
import jax
import jax.numpy as jnp
from jax import lax
from jax.sharding import PartitionSpec as P

NSRC = 4


def shifted(block, offset, n_t):
    pairs = [(t, (t + offset) % n_t) for t in range(n_t)]
    return lax.ppermute(block, "tsink", pairs)


def swapped(block, n_t):
    return lax.ppermute(block, "tsink", [(t, t ^ 1) for t in range(n_t)])


def source_pieces(own_elemental, src_times):
    n_t = lax.axis_size("tsink")
    order = own_elemental.shape[0]
    rows = order // n_t
    half = rows // 2
    pieces = own_elemental.reshape(n_t, rows, order)
    received = lax.all_to_all(pieces, "tsink", 0, 0)
    own = received[src_times]
    t = lax.axis_index("tsink")
    step = 2
    partner = swapped(own, n_t)
    from_left = shifted(own, step, n_t)
    from_right = shifted(own, -step, n_t)
    far = jnp.concatenate(
        [shifted(from_left[:, :half], step, n_t), shifted(from_right[:, half:], -step, n_t)], axis=1
    )
    partner_left = shifted(partner, step, n_t)
    partner_right = shifted(partner, -step, n_t)
    partner_far = jnp.concatenate(
        [shifted(partner_left[:, :half], step, n_t), shifted(partner_right[:, half:], -step, n_t)],
        axis=1,
    )
    return [
        (t, own),
        (t ^ 1, partner),
        ((t - step) % n_t, from_left),
        ((t + step) % n_t, from_right),
        ((t + 2 * step) % n_t, far),
        ((t - step) % n_t ^ 1, partner_left),
        ((t + step) % n_t ^ 1, partner_right),
        ((t + 2 * step) % n_t ^ 1, partner_far),
    ]


def body(perambulators, elementals, src_times, diagrams):
    propagators = perambulators[0]
    own_elemental = elementals[0, 0]
    block_order = propagators.shape[1]
    pieces = source_pieces(own_elemental, src_times)
    rows = pieces[0][1].shape[1]
    halves = jnp.zeros((NSRC, block_order, block_order), jnp.bfloat16)
    for origin, piece in pieces:
        block = jnp.einsum(
            "sik,sjk->sij", piece, propagators, preferred_element_type=jnp.float32
        ).astype(jnp.bfloat16)
        halves = lax.dynamic_update_slice_in_dim(halves, block, origin * rows, 1)
    summed = jnp.zeros((block_order, block_order), jnp.float32)
    for source in range(NSRC):
        summed = summed + jnp.dot(
            propagators[source], halves[source], preferred_element_type=jnp.float32
        )
    meson = summed.astype(jnp.bfloat16)

    n_m = lax.axis_size("mom")
    width = 128
    n_b = block_order // width
    grid = meson.reshape(n_b, width, n_b, width).transpose(0, 2, 1, 3).reshape(n_b * n_b, width, width)
    pairs = [(row, col) for col in range(n_b) for row in range(col + 1)]
    upper = grid[np.array([row * n_b + col for row, col in pairs])]
    upper_t = jnp.swapaxes(grid[np.array([col * n_b + row for row, col in pairs])], 1, 2)
    row_index = lax.broadcasted_iota(jnp.int32, (width, width), 0)
    col_index = lax.broadcasted_iota(jnp.int32, (width, width), 1)
    triangle = jnp.where(row_index < col_index, 1.0, jnp.where(row_index == col_index, 0.5, 0.0))
    on_diagonal = np.array([row == col for row, col in pairs])[:, None, None]
    weight = jnp.where(on_diagonal, triangle[None], 1.0).astype(jnp.bfloat16)
    upper = (upper * weight).reshape(-1, width)
    upper_t = upper_t.reshape(-1, width)
    share = upper.shape[0] // n_m
    slices = jnp.concatenate(
        [upper.reshape(n_m, share, width), upper_t.reshape(n_m, share, width)], axis=1
    )
    received = lax.all_to_all(slices, "mom", 0, 0)
    own_rows = received[:, :share].reshape(n_m, share * width)
    own_cols = received[:, share:].reshape(n_m, share * width)
    partial = lax.dot_general(
        own_rows, own_cols, (((1,), (1,)), ((), ())), preferred_element_type=jnp.float32
    )
    partial = partial + partial.T
    per_diagram = partial[diagrams[:, 0], diagrams[:, 1]]
    spread = lax.all_to_all(per_diagram.reshape(n_m, -1), "mom", 0, 0)
    correlators = (jnp.sum(spread, axis=0) / block_order)[:, None]
    return (meson[None, None], correlators)


def solution(mesh):
    in_specs = (P("tsink", None, None, None), P("tsink", "mom", None, None), P(), P())
    out_specs = (P("tsink", "mom", None, None), P("mom", "tsink"))
    return jax.shard_map(body, mesh=mesh, in_specs=in_specs, out_specs=out_specs, check_vma=False)
```

```python
import numpy as np
import jax
import jax.numpy as jnp
from jax import lax
from jax.sharding import PartitionSpec as P

NSRC = 4


def shifted(block, offset, n_t):
    pairs = [(t, (t + offset) % n_t) for t in range(n_t)]
    return lax.ppermute(block, "tsink", pairs)


def swapped(block, n_t):
    return lax.ppermute(block, "tsink", [(t, t ^ 1) for t in range(n_t)])


def source_pieces(own_elemental, src_times):
    n_t = lax.axis_size("tsink")
    order = own_elemental.shape[0]
    rows = order // n_t
    half = rows // 2
    quarter = half // 2
    pieces = own_elemental.reshape(n_t, rows, order)
    received = lax.all_to_all(pieces, "tsink", 0, 0)
    own = received[src_times]
    t = lax.axis_index("tsink")
    step = 2
    partner = swapped(own, n_t)
    from_left = shifted(own, step, n_t)
    from_right = shifted(own, -step, n_t)
    far = jnp.concatenate(
        [shifted(from_left[:, :half], step, n_t), shifted(from_right[:, half:], -step, n_t)], axis=1
    )
    partner_b = swapped(jnp.stack([from_left[:, half:], from_right[:, half:]]), n_t)
    partner_left_a = shifted(partner[:, :half], step, n_t)
    partner_right_a = shifted(partner[:, :half], -step, n_t)
    partner_far_a = jnp.concatenate(
        [
            shifted(partner_left_a[:, :quarter], step, n_t),
            shifted(partner_right_a[:, quarter:], -step, n_t),
        ],
        axis=1,
    )
    partner_far_b = swapped(far[:, half:], n_t)
    return [
        (t, own),
        (t ^ 1, partner),
        ((t - step) % n_t, from_left),
        ((t + step) % n_t, from_right),
        ((t + 2 * step) % n_t, far),
        ((t - step) % n_t ^ 1, jnp.concatenate([partner_left_a, partner_b[0]], axis=1)),
        ((t + step) % n_t ^ 1, jnp.concatenate([partner_right_a, partner_b[1]], axis=1)),
        ((t + 2 * step) % n_t ^ 1, jnp.concatenate([partner_far_a, partner_far_b], axis=1)),
    ]


def body(perambulators, elementals, src_times, diagrams):
    propagators = perambulators[0]
    own_elemental = elementals[0, 0]
    block_order = propagators.shape[1]
    pieces = source_pieces(own_elemental, src_times)
    rows = pieces[0][1].shape[1]
    halves = jnp.zeros((NSRC, block_order, block_order), jnp.bfloat16)
    for origin, piece in pieces:
        block = jnp.einsum(
            "sik,sjk->sij", piece, propagators, preferred_element_type=jnp.float32
        ).astype(jnp.bfloat16)
        halves = lax.dynamic_update_slice_in_dim(halves, block, origin * rows, 1)
    summed = jnp.zeros((block_order, block_order), jnp.float32)
    for source in range(NSRC):
        summed = summed + jnp.dot(
            propagators[source], halves[source], preferred_element_type=jnp.float32
        )
    meson = summed.astype(jnp.bfloat16)

    n_m = lax.axis_size("mom")
    width = 128
    n_b = block_order // width
    grid = meson.reshape(n_b, width, n_b, width).transpose(0, 2, 1, 3).reshape(n_b * n_b, width, width)
    pairs = [(row, col) for col in range(n_b) for row in range(col + 1)]
    upper = grid[np.array([row * n_b + col for row, col in pairs])]
    upper_t = jnp.swapaxes(grid[np.array([col * n_b + row for row, col in pairs])], 1, 2)
    row_index = lax.broadcasted_iota(jnp.int32, (width, width), 0)
    col_index = lax.broadcasted_iota(jnp.int32, (width, width), 1)
    triangle = jnp.where(row_index < col_index, 1.0, jnp.where(row_index == col_index, 0.5, 0.0))
    on_diagonal = np.array([row == col for row, col in pairs])[:, None, None]
    weight = jnp.where(on_diagonal, triangle[None], 1.0).astype(jnp.bfloat16)
    upper = (upper * weight).reshape(-1, width)
    upper_t = upper_t.reshape(-1, width)
    share = upper.shape[0] // n_m
    slices = jnp.concatenate(
        [upper.reshape(n_m, share, width), upper_t.reshape(n_m, share, width)], axis=1
    )
    received = lax.all_to_all(slices, "mom", 0, 0)
    own_rows = received[:, :share].reshape(n_m, share * width)
    own_cols = received[:, share:].reshape(n_m, share * width)
    partial = lax.dot_general(
        own_rows, own_cols, (((1,), (1,)), ((), ())), preferred_element_type=jnp.float32
    )
    partial = partial + partial.T
    per_diagram = partial[diagrams[:, 0], diagrams[:, 1]]
    spread = lax.all_to_all(per_diagram.reshape(n_m, -1), "mom", 0, 0)
    correlators = (jnp.sum(spread, axis=0) / block_order)[:, None]
    return (meson[None, None], correlators)


def solution(mesh):
    in_specs = (P("tsink", None, None, None), P("tsink", "mom", None, None), P(), P())
    out_specs = (P("tsink", "mom", None, None), P("mom", "tsink"))
    return jax.shard_map(body, mesh=mesh, in_specs=in_specs, out_specs=out_specs, check_vma=False)
```

```python
import numpy as np
import jax
import jax.numpy as jnp
from jax import lax
from jax.sharding import PartitionSpec as P

NSRC = 4


def shifted(block, offset, n_t):
    pairs = [(t, (t + offset) % n_t) for t in range(n_t)]
    return lax.ppermute(block, "tsink", pairs)


def swapped(block, n_t):
    return lax.ppermute(block, "tsink", [(t, t ^ 1) for t in range(n_t)])


def source_pieces(own_elemental, src_times):
    n_t = lax.axis_size("tsink")
    order = own_elemental.shape[0]
    rows = order // n_t
    half = rows // 2
    quarter = half // 2
    pieces = own_elemental.reshape(n_t, rows, order)
    received = lax.all_to_all(pieces, "tsink", 0, 0)
    own = received[src_times]
    t = lax.axis_index("tsink")
    step = 2
    partner = swapped(own, n_t)
    from_left = shifted(own, step, n_t)
    from_right = shifted(own, -step, n_t)
    far = jnp.concatenate(
        [shifted(from_left[:, :half], step, n_t), shifted(from_right[:, half:], -step, n_t)], axis=1
    )
    partner_b = swapped(jnp.stack([from_left[:, half:], from_right[:, half:]]), n_t)
    partner_left_a = shifted(partner[:, :half], step, n_t)
    partner_right_a = shifted(partner[:, :half], -step, n_t)
    partner_far_a = jnp.concatenate(
        [
            shifted(partner_left_a[:, :quarter], step, n_t),
            shifted(partner_right_a[:, quarter:], -step, n_t),
        ],
        axis=1,
    )
    partner_far_b = swapped(far[:, half:], n_t)
    return [
        (t, own),
        (t ^ 1, partner),
        ((t - step) % n_t, from_left),
        ((t + step) % n_t, from_right),
        ((t + 2 * step) % n_t, far),
        ((t - step) % n_t ^ 1, jnp.concatenate([partner_left_a, partner_b[0]], axis=1)),
        ((t + step) % n_t ^ 1, jnp.concatenate([partner_right_a, partner_b[1]], axis=1)),
        ((t + 2 * step) % n_t ^ 1, jnp.concatenate([partner_far_a, partner_far_b], axis=1)),
    ]


def body(perambulators, elementals, src_times, diagrams):
    propagators = perambulators[0]
    own_elemental = elementals[0, 0]
    block_order = propagators.shape[1]
    pieces = source_pieces(own_elemental, src_times)
    rows = pieces[0][1].shape[1]
    halves = jnp.zeros((NSRC, block_order, block_order), jnp.bfloat16)
    for origin, piece in pieces:
        block = jnp.einsum(
            "sik,sjk->sij", piece, propagators, preferred_element_type=jnp.float32
        ).astype(jnp.bfloat16)
        halves = lax.dynamic_update_slice_in_dim(halves, block, origin * rows, 1)
    summed = jnp.einsum("sik,skj->ij", propagators, halves, preferred_element_type=jnp.float32)
    meson = summed.astype(jnp.bfloat16)

    n_m = lax.axis_size("mom")
    width = 128
    n_b = block_order // width
    grid = meson.reshape(n_b, width, n_b, width).transpose(0, 2, 1, 3).reshape(n_b * n_b, width, width)
    pairs = [(row, col) for col in range(n_b) for row in range(col + 1)]
    upper = grid[np.array([row * n_b + col for row, col in pairs])]
    upper_t = jnp.swapaxes(grid[np.array([col * n_b + row for row, col in pairs])], 1, 2)
    row_index = lax.broadcasted_iota(jnp.int32, (width, width), 0)
    col_index = lax.broadcasted_iota(jnp.int32, (width, width), 1)
    triangle = jnp.where(row_index < col_index, 1.0, jnp.where(row_index == col_index, 0.5, 0.0))
    on_diagonal = np.array([row == col for row, col in pairs])[:, None, None]
    weight = jnp.where(on_diagonal, triangle[None], 1.0).astype(jnp.bfloat16)
    upper = (upper * weight).reshape(-1, width)
    upper_t = upper_t.reshape(-1, width)
    share = upper.shape[0] // n_m
    slices = jnp.concatenate(
        [upper.reshape(n_m, share, width), upper_t.reshape(n_m, share, width)], axis=1
    )
    received = lax.all_to_all(slices, "mom", 0, 0)
    own_rows = received[:, :share].reshape(n_m, share * width)
    own_cols = received[:, share:].reshape(n_m, share * width)
    partial = lax.dot_general(
        own_rows, own_cols, (((1,), (1,)), ((), ())), preferred_element_type=jnp.float32
    )
    partial = partial + partial.T
    per_diagram = partial[diagrams[:, 0], diagrams[:, 1]]
    spread = lax.all_to_all(per_diagram.reshape(n_m, -1), "mom", 0, 0)
    correlators = (jnp.sum(spread, axis=0) / block_order)[:, None]
    return (meson[None, None], correlators)


def solution(mesh):
    in_specs = (P("tsink", None, None, None), P("tsink", "mom", None, None), P(), P())
    out_specs = (P("tsink", "mom", None, None), P("mom", "tsink"))
    return jax.shard_map(body, mesh=mesh, in_specs=in_specs, out_specs=out_specs, check_vma=False)
```

```python
import numpy as np
import jax
import jax.numpy as jnp
from jax import lax
from jax.sharding import PartitionSpec as P

NSRC = 4


def shifted(block, offset, n_t):
    pairs = [(t, (t + offset) % n_t) for t in range(n_t)]
    return lax.ppermute(block, "tsink", pairs)


def swapped(block, n_t):
    return lax.ppermute(block, "tsink", [(t, t ^ 1) for t in range(n_t)])


def source_pieces(own):
    n_t = lax.axis_size("tsink")
    rows = own.shape[1]
    half = rows // 2
    quarter = half // 2
    t = lax.axis_index("tsink")
    step = 2
    partner = swapped(own, n_t)
    from_left = shifted(own, step, n_t)
    from_right = shifted(own, -step, n_t)
    far = jnp.concatenate(
        [shifted(from_left[:, :half], step, n_t), shifted(from_right[:, half:], -step, n_t)], axis=1
    )
    partner_b = swapped(jnp.stack([from_left[:, half:], from_right[:, half:]]), n_t)
    partner_left_a = shifted(partner[:, :half], step, n_t)
    partner_right_a = shifted(partner[:, :half], -step, n_t)
    partner_far_a = jnp.concatenate(
        [
            shifted(partner_left_a[:, :quarter], step, n_t),
            shifted(partner_right_a[:, quarter:], -step, n_t),
        ],
        axis=1,
    )
    partner_far_b = swapped(far[:, half:], n_t)
    return [
        (t, own),
        (t ^ 1, partner),
        ((t - step) % n_t, from_left),
        ((t + step) % n_t, from_right),
        ((t + 2 * step) % n_t, far),
        ((t - step) % n_t ^ 1, jnp.concatenate([partner_left_a, partner_b[0]], axis=1)),
        ((t + step) % n_t ^ 1, jnp.concatenate([partner_right_a, partner_b[1]], axis=1)),
        ((t + 2 * step) % n_t ^ 1, jnp.concatenate([partner_far_a, partner_far_b], axis=1)),
    ]


def body(perambulators, elementals, src_times, diagrams):
    propagators = perambulators[0]
    own_elemental = elementals[0, 0]
    block_order = propagators.shape[1]
    n_t = lax.axis_size("tsink")
    rows = block_order // n_t
    received = lax.all_to_all(own_elemental.reshape(n_t, rows, block_order), "tsink", 0, 0)
    chosen = received[src_times]
    summed = jnp.zeros((block_order, block_order), jnp.float32)
    group = NSRC // 2
    for first in range(0, NSRC, group):
        sources = propagators[first:first + group]
        halves = jnp.zeros((group, block_order, block_order), jnp.bfloat16)
        for origin, piece in source_pieces(chosen[first:first + group]):
            block = jnp.einsum(
                "sik,sjk->sij", piece, sources, preferred_element_type=jnp.float32
            ).astype(jnp.bfloat16)
            halves = lax.dynamic_update_slice_in_dim(halves, block, origin * rows, 1)
        for source in range(group):
            summed = summed + jnp.dot(
                sources[source], halves[source], preferred_element_type=jnp.float32
            )
    meson = summed.astype(jnp.bfloat16)

    n_m = lax.axis_size("mom")
    width = 128
    n_b = block_order // width
    grid = meson.reshape(n_b, width, n_b, width).transpose(0, 2, 1, 3).reshape(n_b * n_b, width, width)
    pairs = [(row, col) for col in range(n_b) for row in range(col + 1)]
    upper = grid[np.array([row * n_b + col for row, col in pairs])]
    upper_t = jnp.swapaxes(grid[np.array([col * n_b + row for row, col in pairs])], 1, 2)
    row_index = lax.broadcasted_iota(jnp.int32, (width, width), 0)
    col_index = lax.broadcasted_iota(jnp.int32, (width, width), 1)
    triangle = jnp.where(row_index < col_index, 1.0, jnp.where(row_index == col_index, 0.5, 0.0))
    on_diagonal = np.array([row == col for row, col in pairs])[:, None, None]
    weight = jnp.where(on_diagonal, triangle[None], 1.0).astype(jnp.bfloat16)
    upper = (upper * weight).reshape(-1, width)
    upper_t = upper_t.reshape(-1, width)
    share = upper.shape[0] // n_m
    slices = jnp.concatenate(
        [upper.reshape(n_m, share, width), upper_t.reshape(n_m, share, width)], axis=1
    )
    received = lax.all_to_all(slices, "mom", 0, 0)
    own_rows = received[:, :share].reshape(n_m, share * width)
    own_cols = received[:, share:].reshape(n_m, share * width)
    partial = lax.dot_general(
        own_rows, own_cols, (((1,), (1,)), ((), ())), preferred_element_type=jnp.float32
    )
    partial = partial + partial.T
    per_diagram = partial[diagrams[:, 0], diagrams[:, 1]]
    spread = lax.all_to_all(per_diagram.reshape(n_m, -1), "mom", 0, 0)
    correlators = (jnp.sum(spread, axis=0) / block_order)[:, None]
    return (meson[None, None], correlators)


def solution(mesh):
    in_specs = (P("tsink", None, None, None), P("tsink", "mom", None, None), P(), P())
    out_specs = (P("tsink", "mom", None, None), P("mom", "tsink"))
    return jax.shard_map(body, mesh=mesh, in_specs=in_specs, out_specs=out_specs, check_vma=False)
```

```python
import numpy as np
import jax
import jax.numpy as jnp
from jax import lax
from jax.sharding import PartitionSpec as P

NSRC = 4


def shifted(block, offset, n_t):
    pairs = [(t, (t + offset) % n_t) for t in range(n_t)]
    return lax.ppermute(block, "tsink", pairs)


def swapped(block, n_t):
    return lax.ppermute(block, "tsink", [(t, t ^ 1) for t in range(n_t)])


def source_pieces(own_elemental, src_times):
    n_t = lax.axis_size("tsink")
    order = own_elemental.shape[0]
    rows = order // n_t
    half = rows // 2
    quarter = half // 2
    pieces = own_elemental.reshape(n_t, rows, order)
    received = lax.all_to_all(pieces, "tsink", 0, 0)
    own = received[src_times]
    t = lax.axis_index("tsink")
    step = 2
    partner = swapped(own, n_t)
    from_left = shifted(own, step, n_t)
    from_right = shifted(own, -step, n_t)
    to_right = shifted(jnp.stack([from_left[:, :half], partner[:, :half]]), step, n_t)
    to_left = shifted(jnp.stack([from_right[:, half:], partner[:, :half]]), -step, n_t)
    far = jnp.concatenate([to_right[0], to_left[0]], axis=1)
    partner_b = swapped(jnp.stack([from_left[:, half:], from_right[:, half:]]), n_t)
    partner_left_a = to_right[1]
    partner_right_a = to_left[1]
    partner_far_a = jnp.concatenate(
        [
            shifted(partner_left_a[:, :quarter], step, n_t),
            shifted(partner_right_a[:, quarter:], -step, n_t),
        ],
        axis=1,
    )
    partner_far_b = swapped(far[:, half:], n_t)
    return [
        (t, own),
        (t ^ 1, partner),
        ((t - step) % n_t, from_left),
        ((t + step) % n_t, from_right),
        ((t + 2 * step) % n_t, far),
        ((t - step) % n_t ^ 1, jnp.concatenate([partner_left_a, partner_b[0]], axis=1)),
        ((t + step) % n_t ^ 1, jnp.concatenate([partner_right_a, partner_b[1]], axis=1)),
        ((t + 2 * step) % n_t ^ 1, jnp.concatenate([partner_far_a, partner_far_b], axis=1)),
    ]


def body(perambulators, elementals, src_times, diagrams):
    propagators = perambulators[0]
    own_elemental = elementals[0, 0]
    block_order = propagators.shape[1]
    pieces = source_pieces(own_elemental, src_times)
    rows = pieces[0][1].shape[1]
    halves = jnp.zeros((NSRC, block_order, block_order), jnp.bfloat16)
    for origin, piece in pieces:
        block = jnp.einsum(
            "sik,sjk->sij", piece, propagators, preferred_element_type=jnp.float32
        ).astype(jnp.bfloat16)
        halves = lax.dynamic_update_slice_in_dim(halves, block, origin * rows, 1)
    summed = jnp.zeros((block_order, block_order), jnp.float32)
    for source in range(NSRC):
        summed = summed + jnp.dot(
            propagators[source], halves[source], preferred_element_type=jnp.float32
        )
    meson = summed.astype(jnp.bfloat16)

    n_m = lax.axis_size("mom")
    width = 128
    n_b = block_order // width
    grid = meson.reshape(n_b, width, n_b, width).transpose(0, 2, 1, 3).reshape(n_b * n_b, width, width)
    pairs = [(row, col) for col in range(n_b) for row in range(col + 1)]
    upper = grid[np.array([row * n_b + col for row, col in pairs])]
    upper_t = jnp.swapaxes(grid[np.array([col * n_b + row for row, col in pairs])], 1, 2)
    row_index = lax.broadcasted_iota(jnp.int32, (width, width), 0)
    col_index = lax.broadcasted_iota(jnp.int32, (width, width), 1)
    triangle = jnp.where(row_index < col_index, 1.0, jnp.where(row_index == col_index, 0.5, 0.0))
    on_diagonal = np.array([row == col for row, col in pairs])[:, None, None]
    weight = jnp.where(on_diagonal, triangle[None], 1.0).astype(jnp.bfloat16)
    upper = (upper * weight).reshape(-1, width)
    upper_t = upper_t.reshape(-1, width)
    share = upper.shape[0] // n_m
    slices = jnp.concatenate(
        [upper.reshape(n_m, share, width), upper_t.reshape(n_m, share, width)], axis=1
    )
    received = lax.all_to_all(slices, "mom", 0, 0)
    own_rows = received[:, :share].reshape(n_m, share * width)
    own_cols = received[:, share:].reshape(n_m, share * width)
    partial = lax.dot_general(
        own_rows, own_cols, (((1,), (1,)), ((), ())), preferred_element_type=jnp.float32
    )
    partial = partial + partial.T
    per_diagram = partial[diagrams[:, 0], diagrams[:, 1]]
    spread = lax.all_to_all(per_diagram.reshape(n_m, -1), "mom", 0, 0)
    correlators = (jnp.sum(spread, axis=0) / block_order)[:, None]
    return (meson[None, None], correlators)


def solution(mesh):
    in_specs = (P("tsink", None, None, None), P("tsink", "mom", None, None), P(), P())
    out_specs = (P("tsink", "mom", None, None), P("mom", "tsink"))
    return jax.shard_map(body, mesh=mesh, in_specs=in_specs, out_specs=out_specs, check_vma=False)
```

```python
import numpy as np
import jax
import jax.numpy as jnp
from jax import lax
from jax.sharding import PartitionSpec as P

NSRC = 4


def shifted(block, offset, n_t):
    pairs = [(t, (t + offset) % n_t) for t in range(n_t)]
    return lax.ppermute(block, "tsink", pairs)


def swapped(block, n_t):
    return lax.ppermute(block, "tsink", [(t, t ^ 1) for t in range(n_t)])


def source_pieces(own_elemental, src_times):
    n_t = lax.axis_size("tsink")
    order = own_elemental.shape[0]
    rows = order // n_t
    half = rows // 2
    quarter = half // 2
    pieces = own_elemental.reshape(n_t, rows, order)
    received = lax.all_to_all(pieces, "tsink", 0, 0)
    own = received[src_times]
    t = lax.axis_index("tsink")
    step = 2
    partner = swapped(own, n_t)
    from_left = shifted(own, step, n_t)
    from_right = shifted(own, -step, n_t)
    to_right = shifted(jnp.stack([from_left[:, :half], partner[:, :half]]), step, n_t)
    to_left = shifted(jnp.stack([from_right[:, half:], partner[:, :half]]), -step, n_t)
    far = jnp.concatenate([to_right[0], to_left[0]], axis=1)
    partner_b = swapped(jnp.stack([from_left[:, half:], from_right[:, half:]]), n_t)
    partner_left_a = to_right[1]
    partner_right_a = to_left[1]
    partner_far_a = jnp.concatenate(
        [
            shifted(partner_left_a[:, :quarter], step, n_t),
            shifted(partner_right_a[:, quarter:], -step, n_t),
        ],
        axis=1,
    )
    partner_far_b = swapped(far[:, half:], n_t)
    return [
        (t, own),
        (t ^ 1, partner),
        ((t - step) % n_t, from_left),
        ((t + step) % n_t, from_right),
        ((t + 2 * step) % n_t, far),
        ((t - step) % n_t ^ 1, jnp.concatenate([partner_left_a, partner_b[0]], axis=1)),
        ((t + step) % n_t ^ 1, jnp.concatenate([partner_right_a, partner_b[1]], axis=1)),
        ((t + 2 * step) % n_t ^ 1, jnp.concatenate([partner_far_a, partner_far_b], axis=1)),
    ]


def body(perambulators, elementals, src_times, diagrams):
    propagators = perambulators[0]
    own_elemental = elementals[0, 0]
    block_order = propagators.shape[1]
    pieces = source_pieces(own_elemental, src_times)
    rows = pieces[0][1].shape[1]
    halves = jnp.zeros((NSRC, block_order, block_order), jnp.bfloat16)
    for origin, piece in pieces:
        block = jnp.einsum(
            "sik,sjk->sij", piece, propagators, preferred_element_type=jnp.float32
        ).astype(jnp.bfloat16)
        halves = lax.dynamic_update_slice_in_dim(halves, block, origin * rows, 1)
    side_by_side = jnp.concatenate([propagators[source] for source in range(NSRC)], axis=1)
    summed = jnp.dot(
        side_by_side, halves.reshape(NSRC * block_order, block_order),
        preferred_element_type=jnp.float32,
    )
    meson = summed.astype(jnp.bfloat16)

    n_m = lax.axis_size("mom")
    width = 128
    n_b = block_order // width
    grid = meson.reshape(n_b, width, n_b, width).transpose(0, 2, 1, 3).reshape(n_b * n_b, width, width)
    pairs = [(row, col) for col in range(n_b) for row in range(col + 1)]
    upper = grid[np.array([row * n_b + col for row, col in pairs])]
    upper_t = jnp.swapaxes(grid[np.array([col * n_b + row for row, col in pairs])], 1, 2)
    row_index = lax.broadcasted_iota(jnp.int32, (width, width), 0)
    col_index = lax.broadcasted_iota(jnp.int32, (width, width), 1)
    triangle = jnp.where(row_index < col_index, 1.0, jnp.where(row_index == col_index, 0.5, 0.0))
    on_diagonal = np.array([row == col for row, col in pairs])[:, None, None]
    weight = jnp.where(on_diagonal, triangle[None], 1.0).astype(jnp.bfloat16)
    upper = (upper * weight).reshape(-1, width)
    upper_t = upper_t.reshape(-1, width)
    share = upper.shape[0] // n_m
    slices = jnp.concatenate(
        [upper.reshape(n_m, share, width), upper_t.reshape(n_m, share, width)], axis=1
    )
    received = lax.all_to_all(slices, "mom", 0, 0)
    own_rows = received[:, :share].reshape(n_m, share * width)
    own_cols = received[:, share:].reshape(n_m, share * width)
    partial = lax.dot_general(
        own_rows, own_cols, (((1,), (1,)), ((), ())), preferred_element_type=jnp.float32
    )
    partial = partial + partial.T
    per_diagram = partial[diagrams[:, 0], diagrams[:, 1]]
    spread = lax.all_to_all(per_diagram.reshape(n_m, -1), "mom", 0, 0)
    correlators = (jnp.sum(spread, axis=0) / block_order)[:, None]
    return (meson[None, None], correlators)


def solution(mesh):
    in_specs = (P("tsink", None, None, None), P("tsink", "mom", None, None), P(), P())
    out_specs = (P("tsink", "mom", None, None), P("mom", "tsink"))
    return jax.shard_map(body, mesh=mesh, in_specs=in_specs, out_specs=out_specs, check_vma=False)
```

```python
import numpy as np
import jax
import jax.numpy as jnp
from jax import lax
from jax.sharding import PartitionSpec as P

NSRC = 4


def shifted(block, offset, n_t):
    pairs = [(t, (t + offset) % n_t) for t in range(n_t)]
    return lax.ppermute(block, "tsink", pairs)


def swapped(block, n_t):
    return lax.ppermute(block, "tsink", [(t, t ^ 1) for t in range(n_t)])


def source_pieces(own_elemental, src_times):
    n_t = lax.axis_size("tsink")
    order = own_elemental.shape[0]
    rows = order // n_t
    half = rows // 2
    quarter = half // 2
    pieces = own_elemental.reshape(n_t, rows, order)
    received = lax.all_to_all(pieces, "tsink", 0, 0)
    own = received[src_times]
    t = lax.axis_index("tsink")
    step = 2
    partner = swapped(own, n_t)
    from_left = shifted(own, step, n_t)
    from_right = shifted(own, -step, n_t)
    to_right = shifted(jnp.stack([from_left[:, :half], partner[:, :half]]), step, n_t)
    to_left = shifted(jnp.stack([from_right[:, half:], partner[:, :half]]), -step, n_t)
    far = jnp.concatenate([to_right[0], to_left[0]], axis=1)
    partner_b = swapped(jnp.stack([from_left[:, half:], from_right[:, half:]]), n_t)
    partner_left_a = to_right[1]
    partner_right_a = to_left[1]
    partner_far_a = jnp.concatenate(
        [
            shifted(partner_left_a[:, :quarter], step, n_t),
            shifted(partner_right_a[:, quarter:], -step, n_t),
        ],
        axis=1,
    )
    partner_far_b = swapped(far[:, half:], n_t)
    return [
        (t, own),
        (t ^ 1, partner),
        ((t - step) % n_t, from_left),
        ((t + step) % n_t, from_right),
        ((t + 2 * step) % n_t, far),
        ((t - step) % n_t ^ 1, jnp.concatenate([partner_left_a, partner_b[0]], axis=1)),
        ((t + step) % n_t ^ 1, jnp.concatenate([partner_right_a, partner_b[1]], axis=1)),
        ((t + 2 * step) % n_t ^ 1, jnp.concatenate([partner_far_a, partner_far_b], axis=1)),
    ]


def body(perambulators, elementals, src_times, diagrams):
    propagators = perambulators[0]
    own_elemental = elementals[0, 0]
    block_order = propagators.shape[1]
    pieces = source_pieces(own_elemental, src_times)
    rows = pieces[0][1].shape[1]
    def stacked(group):
        columns = jnp.concatenate(
            [
                lax.dynamic_slice_in_dim(propagators[source], origin * rows, rows, 1)
                for source in range(NSRC)
                for origin, _ in group
            ],
            axis=1,
        )
        blocks = jnp.stack(
            [
                jnp.einsum(
                    "sik,sjk->sij", piece, propagators, preferred_element_type=jnp.float32
                ).astype(jnp.bfloat16)
                for _, piece in group
            ],
            axis=1,
        )
        return jnp.dot(
            columns, blocks.reshape(-1, block_order), preferred_element_type=jnp.float32
        )

    summed = stacked(pieces[:4]) + stacked(pieces[4:])
    meson = summed.astype(jnp.bfloat16)

    n_m = lax.axis_size("mom")
    width = 128
    n_b = block_order // width
    grid = meson.reshape(n_b, width, n_b, width).transpose(0, 2, 1, 3).reshape(n_b * n_b, width, width)
    pairs = [(row, col) for col in range(n_b) for row in range(col + 1)]
    upper = grid[np.array([row * n_b + col for row, col in pairs])]
    upper_t = jnp.swapaxes(grid[np.array([col * n_b + row for row, col in pairs])], 1, 2)
    row_index = lax.broadcasted_iota(jnp.int32, (width, width), 0)
    col_index = lax.broadcasted_iota(jnp.int32, (width, width), 1)
    triangle = jnp.where(row_index < col_index, 1.0, jnp.where(row_index == col_index, 0.5, 0.0))
    on_diagonal = np.array([row == col for row, col in pairs])[:, None, None]
    weight = jnp.where(on_diagonal, triangle[None], 1.0).astype(jnp.bfloat16)
    upper = (upper * weight).reshape(-1, width)
    upper_t = upper_t.reshape(-1, width)
    share = upper.shape[0] // n_m
    slices = jnp.concatenate(
        [upper.reshape(n_m, share, width), upper_t.reshape(n_m, share, width)], axis=1
    )
    received = lax.all_to_all(slices, "mom", 0, 0)
    own_rows = received[:, :share].reshape(n_m, share * width)
    own_cols = received[:, share:].reshape(n_m, share * width)
    partial = lax.dot_general(
        own_rows, own_cols, (((1,), (1,)), ((), ())), preferred_element_type=jnp.float32
    )
    partial = partial + partial.T
    per_diagram = partial[diagrams[:, 0], diagrams[:, 1]]
    spread = lax.all_to_all(per_diagram.reshape(n_m, -1), "mom", 0, 0)
    correlators = (jnp.sum(spread, axis=0) / block_order)[:, None]
    return (meson[None, None], correlators)


def solution(mesh):
    in_specs = (P("tsink", None, None, None), P("tsink", "mom", None, None), P(), P())
    out_specs = (P("tsink", "mom", None, None), P("mom", "tsink"))
    return jax.shard_map(body, mesh=mesh, in_specs=in_specs, out_specs=out_specs, check_vma=False)
```

```python
import numpy as np
import jax
import jax.numpy as jnp
from jax import lax
from jax.sharding import PartitionSpec as P

NSRC = 4


def shifted(block, offset, n_t):
    pairs = [(t, (t + offset) % n_t) for t in range(n_t)]
    return lax.ppermute(block, "tsink", pairs)


def swapped(block, n_t):
    return lax.ppermute(block, "tsink", [(t, t ^ 1) for t in range(n_t)])


def source_pieces(own_elemental, src_times):
    n_t = lax.axis_size("tsink")
    order = own_elemental.shape[0]
    rows = order // n_t
    half = rows // 2
    quarter = half // 2
    pieces = own_elemental.reshape(n_t, rows, order)
    received = lax.all_to_all(pieces, "tsink", 0, 0)
    own = received[src_times]
    t = lax.axis_index("tsink")
    step = 2
    partner = swapped(own, n_t)
    from_left = shifted(own, step, n_t)
    from_right = shifted(own, -step, n_t)
    to_right = shifted(jnp.stack([from_left[:, :half], partner[:, :half]]), step, n_t)
    to_left = shifted(jnp.stack([from_right[:, half:], partner[:, :half]]), -step, n_t)
    far = jnp.concatenate([to_right[0], to_left[0]], axis=1)
    partner_b = swapped(jnp.stack([from_left[:, half:], from_right[:, half:]]), n_t)
    partner_left_a = to_right[1]
    partner_right_a = to_left[1]
    partner_far_a = jnp.concatenate(
        [
            shifted(partner_left_a[:, :quarter], step, n_t),
            shifted(partner_right_a[:, quarter:], -step, n_t),
        ],
        axis=1,
    )
    partner_far_b = swapped(far[:, half:], n_t)
    return [
        (t, own),
        (t ^ 1, partner),
        ((t - step) % n_t, from_left),
        ((t + step) % n_t, from_right),
        ((t + 2 * step) % n_t, far),
        ((t - step) % n_t ^ 1, jnp.concatenate([partner_left_a, partner_b[0]], axis=1)),
        ((t + step) % n_t ^ 1, jnp.concatenate([partner_right_a, partner_b[1]], axis=1)),
        ((t + 2 * step) % n_t ^ 1, jnp.concatenate([partner_far_a, partner_far_b], axis=1)),
    ]


def body(perambulators, elementals, src_times, diagrams):
    propagators = perambulators[0]
    own_elemental = elementals[0, 0]
    block_order = propagators.shape[1]
    pieces = source_pieces(own_elemental, src_times)
    rows = pieces[0][1].shape[1]
    def stacked(group):
        columns = jnp.concatenate(
            [
                lax.dynamic_slice_in_dim(propagators[source], origin * rows, rows, 1)
                for origin, _ in group
                for source in range(NSRC)
            ],
            axis=1,
        )
        blocks = jnp.stack(
            [
                jnp.einsum(
                    "sik,sjk->sij", piece, propagators, preferred_element_type=jnp.float32
                ).astype(jnp.bfloat16)
                for _, piece in group
            ]
        )
        return jnp.dot(
            columns, blocks.reshape(-1, block_order), preferred_element_type=jnp.float32
        )

    summed = stacked(pieces[:4]) + stacked(pieces[4:])
    meson = summed.astype(jnp.bfloat16)

    n_m = lax.axis_size("mom")
    width = 128
    n_b = block_order // width
    grid = meson.reshape(n_b, width, n_b, width).transpose(0, 2, 1, 3).reshape(n_b * n_b, width, width)
    pairs = [(row, col) for col in range(n_b) for row in range(col + 1)]
    upper = grid[np.array([row * n_b + col for row, col in pairs])]
    upper_t = jnp.swapaxes(grid[np.array([col * n_b + row for row, col in pairs])], 1, 2)
    row_index = lax.broadcasted_iota(jnp.int32, (width, width), 0)
    col_index = lax.broadcasted_iota(jnp.int32, (width, width), 1)
    triangle = jnp.where(row_index < col_index, 1.0, jnp.where(row_index == col_index, 0.5, 0.0))
    on_diagonal = np.array([row == col for row, col in pairs])[:, None, None]
    weight = jnp.where(on_diagonal, triangle[None], 1.0).astype(jnp.bfloat16)
    upper = (upper * weight).reshape(-1, width)
    upper_t = upper_t.reshape(-1, width)
    share = upper.shape[0] // n_m
    slices = jnp.concatenate(
        [upper.reshape(n_m, share, width), upper_t.reshape(n_m, share, width)], axis=1
    )
    received = lax.all_to_all(slices, "mom", 0, 0)
    own_rows = received[:, :share].reshape(n_m, share * width)
    own_cols = received[:, share:].reshape(n_m, share * width)
    partial = lax.dot_general(
        own_rows, own_cols, (((1,), (1,)), ((), ())), preferred_element_type=jnp.float32
    )
    partial = partial + partial.T
    per_diagram = partial[diagrams[:, 0], diagrams[:, 1]]
    spread = lax.all_to_all(per_diagram.reshape(n_m, -1), "mom", 0, 0)
    correlators = (jnp.sum(spread, axis=0) / block_order)[:, None]
    return (meson[None, None], correlators)


def solution(mesh):
    in_specs = (P("tsink", None, None, None), P("tsink", "mom", None, None), P(), P())
    out_specs = (P("tsink", "mom", None, None), P("mom", "tsink"))
    return jax.shard_map(body, mesh=mesh, in_specs=in_specs, out_specs=out_specs, check_vma=False)
```

```python
import numpy as np
import jax
import jax.numpy as jnp
from jax import lax
from jax.sharding import PartitionSpec as P

NSRC = 4


def shifted(block, offset, n_t):
    pairs = [(t, (t + offset) % n_t) for t in range(n_t)]
    return lax.ppermute(block, "tsink", pairs)


def swapped(block, n_t):
    return lax.ppermute(block, "tsink", [(t, t ^ 1) for t in range(n_t)])


def source_pieces(own_elemental, src_times):
    n_t = lax.axis_size("tsink")
    order = own_elemental.shape[0]
    rows = order // n_t
    half = rows // 2
    quarter = half // 2
    pieces = own_elemental.reshape(n_t, rows, order)
    received = lax.all_to_all(pieces, "tsink", 0, 0)
    own = jnp.stack([lax.dynamic_index_in_dim(received, time, 0, False) for time in src_times])
    t = lax.axis_index("tsink")
    step = 2
    partner = swapped(own, n_t)
    from_left = shifted(own, step, n_t)
    from_right = shifted(own, -step, n_t)
    to_right = shifted(jnp.stack([from_left[:, :half], partner[:, :half]]), step, n_t)
    to_left = shifted(jnp.stack([from_right[:, half:], partner[:, :half]]), -step, n_t)
    far = jnp.concatenate([to_right[0], to_left[0]], axis=1)
    partner_b = swapped(jnp.stack([from_left[:, half:], from_right[:, half:]]), n_t)
    partner_left_a = to_right[1]
    partner_right_a = to_left[1]
    partner_far_a = jnp.concatenate(
        [
            shifted(partner_left_a[:, :quarter], step, n_t),
            shifted(partner_right_a[:, quarter:], -step, n_t),
        ],
        axis=1,
    )
    partner_far_b = swapped(far[:, half:], n_t)
    return [
        (t, own),
        (t ^ 1, partner),
        ((t - step) % n_t, from_left),
        ((t + step) % n_t, from_right),
        ((t + 2 * step) % n_t, far),
        ((t - step) % n_t ^ 1, jnp.concatenate([partner_left_a, partner_b[0]], axis=1)),
        ((t + step) % n_t ^ 1, jnp.concatenate([partner_right_a, partner_b[1]], axis=1)),
        ((t + 2 * step) % n_t ^ 1, jnp.concatenate([partner_far_a, partner_far_b], axis=1)),
    ]


def body(perambulators, elementals, src_times, diagrams):
    propagators = perambulators[0]
    own_elemental = elementals[0, 0]
    block_order = propagators.shape[1]
    pieces = source_pieces(own_elemental, src_times)
    rows = pieces[0][1].shape[1]
    def stacked(group):
        columns = jnp.concatenate(
            [
                lax.dynamic_slice_in_dim(propagators[source], origin * rows, rows, 1)
                for origin, _ in group
                for source in range(NSRC)
            ],
            axis=1,
        )
        blocks = jnp.stack(
            [
                jnp.einsum(
                    "sik,sjk->sij", piece, propagators, preferred_element_type=jnp.float32
                ).astype(jnp.bfloat16)
                for _, piece in group
            ]
        )
        return jnp.dot(
            columns, blocks.reshape(-1, block_order), preferred_element_type=jnp.float32
        )

    summed = stacked(pieces[:4]) + stacked(pieces[4:])
    meson = summed.astype(jnp.bfloat16)

    n_m = lax.axis_size("mom")
    width = 128
    n_b = block_order // width
    grid = meson.reshape(n_b, width, n_b, width).transpose(0, 2, 1, 3).reshape(n_b * n_b, width, width)
    pairs = [(row, col) for col in range(n_b) for row in range(col + 1)]
    upper = grid[np.array([row * n_b + col for row, col in pairs])]
    upper_t = jnp.swapaxes(grid[np.array([col * n_b + row for row, col in pairs])], 1, 2)
    row_index = lax.broadcasted_iota(jnp.int32, (width, width), 0)
    col_index = lax.broadcasted_iota(jnp.int32, (width, width), 1)
    triangle = jnp.where(row_index < col_index, 1.0, jnp.where(row_index == col_index, 0.5, 0.0))
    on_diagonal = np.array([row == col for row, col in pairs])[:, None, None]
    weight = jnp.where(on_diagonal, triangle[None], 1.0).astype(jnp.bfloat16)
    upper = (upper * weight).reshape(-1, width)
    upper_t = upper_t.reshape(-1, width)
    share = upper.shape[0] // n_m
    slices = jnp.concatenate(
        [upper.reshape(n_m, share, width), upper_t.reshape(n_m, share, width)], axis=1
    )
    received = lax.all_to_all(slices, "mom", 0, 0)
    own_rows = received[:, :share].reshape(n_m, share * width)
    own_cols = received[:, share:].reshape(n_m, share * width)
    partial = lax.dot_general(
        own_rows, own_cols, (((1,), (1,)), ((), ())), preferred_element_type=jnp.float32
    )
    per_diagram = partial[diagrams[:, 0], diagrams[:, 1]] + partial[diagrams[:, 1], diagrams[:, 0]]
    spread = lax.all_to_all(per_diagram.reshape(n_m, -1), "mom", 0, 0)
    correlators = (jnp.sum(spread, axis=0) / block_order)[:, None]
    return (meson[None, None], correlators)


def solution(mesh):
    in_specs = (P("tsink", None, None, None), P("tsink", "mom", None, None), P(), P())
    out_specs = (P("tsink", "mom", None, None), P("mom", "tsink"))
    return jax.shard_map(body, mesh=mesh, in_specs=in_specs, out_specs=out_specs, check_vma=False)
```

```python
import numpy as np
import jax
import jax.numpy as jnp
from jax import lax
from jax.sharding import PartitionSpec as P

NSRC = 4


def shifted(block, offset, n_t):
    pairs = [(t, (t + offset) % n_t) for t in range(n_t)]
    return lax.ppermute(block, "tsink", pairs)


def swapped(block, n_t):
    return lax.ppermute(block, "tsink", [(t, t ^ 1) for t in range(n_t)])


def source_pieces(own_elemental, src_times):
    n_t = lax.axis_size("tsink")
    order = own_elemental.shape[0]
    rows = order // n_t
    half = rows // 2
    quarter = half // 2
    pieces = own_elemental.reshape(n_t, rows, order)
    received = lax.all_to_all(pieces, "tsink", 0, 0)
    own = received[src_times]
    t = lax.axis_index("tsink")
    step = 2
    partner = swapped(own, n_t)
    from_left = shifted(own, step, n_t)
    from_right = shifted(own, -step, n_t)
    to_right = shifted(jnp.stack([from_left[:, :half], partner[:, :half]]), step, n_t)
    to_left = shifted(jnp.stack([from_right[:, half:], partner[:, :half]]), -step, n_t)
    far = jnp.concatenate([to_right[0], to_left[0]], axis=1)
    partner_b = swapped(jnp.stack([from_left[:, half:], from_right[:, half:]]), n_t)
    partner_left_a = to_right[1]
    partner_right_a = to_left[1]
    partner_far_a = jnp.concatenate(
        [
            shifted(partner_left_a[:, :quarter], step, n_t),
            shifted(partner_right_a[:, quarter:], -step, n_t),
        ],
        axis=1,
    )
    partner_far_b = swapped(far[:, half:], n_t)
    return [
        (t, own),
        (t ^ 1, partner),
        ((t - step) % n_t, from_left),
        ((t + step) % n_t, from_right),
        ((t + 2 * step) % n_t, far),
        ((t - step) % n_t ^ 1, jnp.concatenate([partner_left_a, partner_b[0]], axis=1)),
        ((t + step) % n_t ^ 1, jnp.concatenate([partner_right_a, partner_b[1]], axis=1)),
        ((t + 2 * step) % n_t ^ 1, jnp.concatenate([partner_far_a, partner_far_b], axis=1)),
    ]


def body(perambulators, elementals, src_times, diagrams):
    propagators = perambulators[0]
    own_elemental = elementals[0, 0]
    block_order = propagators.shape[1]
    pieces = source_pieces(own_elemental, src_times)
    rows = pieces[0][1].shape[1]
    def stacked(group):
        origins = jnp.stack([origin for origin, _ in group])
        by_block = propagators.reshape(NSRC, block_order, block_order // rows, rows)
        columns = jnp.take(by_block, origins, axis=2, mode="clip")
        columns = columns.transpose(1, 2, 0, 3).reshape(block_order, -1)
        blocks = jnp.stack(
            [
                jnp.einsum(
                    "sik,sjk->sij", piece, propagators, preferred_element_type=jnp.float32
                ).astype(jnp.bfloat16)
                for _, piece in group
            ]
        )
        return jnp.dot(
            columns, blocks.reshape(-1, block_order), preferred_element_type=jnp.float32
        )

    summed = stacked(pieces[:4]) + stacked(pieces[4:])
    meson = summed.astype(jnp.bfloat16)

    n_m = lax.axis_size("mom")
    width = 128
    n_b = block_order // width
    grid = meson.reshape(n_b, width, n_b, width).transpose(0, 2, 1, 3).reshape(n_b * n_b, width, width)
    pairs = [(row, col) for col in range(n_b) for row in range(col + 1)]
    upper = grid[np.array([row * n_b + col for row, col in pairs])]
    upper_t = jnp.swapaxes(grid[np.array([col * n_b + row for row, col in pairs])], 1, 2)
    row_index = lax.broadcasted_iota(jnp.int32, (width, width), 0)
    col_index = lax.broadcasted_iota(jnp.int32, (width, width), 1)
    triangle = jnp.where(row_index < col_index, 1.0, jnp.where(row_index == col_index, 0.5, 0.0))
    on_diagonal = np.array([row == col for row, col in pairs])[:, None, None]
    weight = jnp.where(on_diagonal, triangle[None], 1.0).astype(jnp.bfloat16)
    upper = (upper * weight).reshape(-1, width)
    upper_t = upper_t.reshape(-1, width)
    share = upper.shape[0] // n_m
    slices = jnp.concatenate(
        [upper.reshape(n_m, share, width), upper_t.reshape(n_m, share, width)], axis=1
    )
    received = lax.all_to_all(slices, "mom", 0, 0)
    own_rows = received[:, :share].reshape(n_m, share * width)
    own_cols = received[:, share:].reshape(n_m, share * width)
    partial = lax.dot_general(
        own_rows, own_cols, (((1,), (1,)), ((), ())), preferred_element_type=jnp.float32
    )
    partial = partial + partial.T
    per_diagram = partial[diagrams[:, 0], diagrams[:, 1]]
    spread = lax.all_to_all(per_diagram.reshape(n_m, -1), "mom", 0, 0)
    correlators = (jnp.sum(spread, axis=0) / block_order)[:, None]
    return (meson[None, None], correlators)


def solution(mesh):
    in_specs = (P("tsink", None, None, None), P("tsink", "mom", None, None), P(), P())
    out_specs = (P("tsink", "mom", None, None), P("mom", "tsink"))
    return jax.shard_map(body, mesh=mesh, in_specs=in_specs, out_specs=out_specs, check_vma=False)
```

```python
import numpy as np
import jax
import jax.numpy as jnp
from jax import lax
from jax.sharding import PartitionSpec as P

NSRC = 4


def shifted(block, offset, n_t):
    pairs = [(t, (t + offset) % n_t) for t in range(n_t)]
    return lax.ppermute(block, "tsink", pairs)


def swapped(block, n_t):
    return lax.ppermute(block, "tsink", [(t, t ^ 1) for t in range(n_t)])


def source_pieces(own_elemental, src_times):
    n_t = lax.axis_size("tsink")
    order = own_elemental.shape[0]
    rows = order // n_t
    half = rows // 2
    quarter = half // 2
    pieces = own_elemental.reshape(n_t, rows, order)
    received = lax.all_to_all(pieces, "tsink", 0, 0)
    own = received[src_times]
    t = lax.axis_index("tsink")
    step = 2
    partner = swapped(own, n_t)
    from_left = shifted(own, step, n_t)
    from_right = shifted(own, -step, n_t)
    to_right = shifted(jnp.stack([from_left[:, :half], partner[:, :half]]), step, n_t)
    to_left = shifted(jnp.stack([from_right[:, half:], partner[:, :half]]), -step, n_t)
    far = jnp.concatenate([to_right[0], to_left[0]], axis=1)
    partner_b = swapped(jnp.stack([from_left[:, half:], from_right[:, half:]]), n_t)
    partner_left_a = to_right[1]
    partner_right_a = to_left[1]
    partner_far_a = jnp.concatenate(
        [
            shifted(partner_left_a[:, :quarter], step, n_t),
            shifted(partner_right_a[:, quarter:], -step, n_t),
        ],
        axis=1,
    )
    partner_far_b = swapped(far[:, half:], n_t)
    return [
        (t, own),
        (t ^ 1, partner),
        ((t - step) % n_t, from_left),
        ((t + step) % n_t, from_right),
        ((t + 2 * step) % n_t, far),
        ((t - step) % n_t ^ 1, jnp.concatenate([partner_left_a, partner_b[0]], axis=1)),
        ((t + step) % n_t ^ 1, jnp.concatenate([partner_right_a, partner_b[1]], axis=1)),
        ((t + 2 * step) % n_t ^ 1, jnp.concatenate([partner_far_a, partner_far_b], axis=1)),
    ]


def body(perambulators, elementals, src_times, diagrams):
    propagators = perambulators[0]
    own_elemental = elementals[0, 0]
    block_order = propagators.shape[1]
    pieces = source_pieces(own_elemental, src_times)
    rows = pieces[0][1].shape[1]
    def stacked(group):
        columns = jnp.concatenate(
            [
                lax.dynamic_slice_in_dim(propagators[source], origin * rows, rows, 1)
                for origin, _ in group
                for source in range(NSRC)
            ],
            axis=1,
        )
        blocks = jnp.stack(
            [
                jnp.einsum(
                    "sik,sjk->sij", piece, propagators, preferred_element_type=jnp.float32
                ).astype(jnp.bfloat16)
                for _, piece in group
            ]
        )
        return jnp.dot(
            columns, blocks.reshape(-1, block_order), preferred_element_type=jnp.float32
        )

    summed = stacked(pieces[:4]) + stacked(pieces[4:])
    meson = summed.astype(jnp.bfloat16)

    n_m = lax.axis_size("mom")
    width = 128
    n_b = block_order // width
    grid = meson.reshape(n_b, width, n_b, width).transpose(0, 2, 1, 3).reshape(n_b * n_b, width, width)
    pairs = [(row, col) for col in range(n_b) for row in range(col + 1)]
    upper = grid[np.array([row * n_b + col for row, col in pairs])]
    upper_t = jnp.swapaxes(grid[np.array([col * n_b + row for row, col in pairs])], 1, 2)
    row_index = lax.broadcasted_iota(jnp.int32, (width, width), 0)
    col_index = lax.broadcasted_iota(jnp.int32, (width, width), 1)
    triangle = jnp.where(row_index < col_index, 1.0, jnp.where(row_index == col_index, 0.5, 0.0))
    on_diagonal = np.array([row == col for row, col in pairs])[:, None, None]
    weight = jnp.where(on_diagonal, triangle[None], 1.0).astype(jnp.bfloat16)
    upper = (upper * weight).reshape(-1, width)
    upper_t = upper_t.reshape(-1, width)
    share = upper.shape[0] // n_m
    slices = jnp.concatenate(
        [upper.reshape(n_m, share, width), upper_t.reshape(n_m, share, width)], axis=1
    )
    received = lax.all_to_all(slices, "mom", 0, 0)
    own_rows = received[:, :share].reshape(n_m, share * width)
    own_cols = received[:, share:].reshape(n_m, share * width)
    partial = lax.dot_general(
        own_rows, own_cols, (((1,), (1,)), ((), ())), preferred_element_type=jnp.float32
    )
    first, second = diagrams[:, 0], diagrams[:, 1]
    per_diagram = partial[first, second] + partial[second, first]
    spread = lax.all_to_all(per_diagram.reshape(n_m, -1), "mom", 0, 0)
    correlators = (jnp.sum(spread, axis=0) / block_order)[:, None]
    return (meson[None, None], correlators)


def solution(mesh):
    in_specs = (P("tsink", None, None, None), P("tsink", "mom", None, None), P(), P())
    out_specs = (P("tsink", "mom", None, None), P("mom", "tsink"))
    return jax.shard_map(body, mesh=mesh, in_specs=in_specs, out_specs=out_specs, check_vma=False)
```

```python
import numpy as np
import jax
import jax.numpy as jnp
from jax import lax
from jax.sharding import PartitionSpec as P

NSRC = 4


def shifted(block, offset, n_t):
    pairs = [(t, (t + offset) % n_t) for t in range(n_t)]
    return lax.ppermute(block, "tsink", pairs)


def swapped(block, n_t):
    return lax.ppermute(block, "tsink", [(t, t ^ 1) for t in range(n_t)])


def source_pieces(own_elemental, src_times, ready):
    n_t = lax.axis_size("tsink")
    order = own_elemental.shape[0]
    rows = order // n_t
    half = rows // 2
    quarter = half // 2
    pieces = own_elemental.reshape(n_t, rows, order)
    received = lax.all_to_all(pieces, "tsink", 0, 0)
    received, ready = lax.optimization_barrier((received, ready))
    own = received[src_times]
    t = lax.axis_index("tsink")
    step = 2
    partner = swapped(own, n_t)
    from_left = shifted(own, step, n_t)
    from_right = shifted(own, -step, n_t)
    to_right = shifted(jnp.stack([from_left[:, :half], partner[:, :half]]), step, n_t)
    to_left = shifted(jnp.stack([from_right[:, half:], partner[:, :half]]), -step, n_t)
    far = jnp.concatenate([to_right[0], to_left[0]], axis=1)
    partner_b = swapped(jnp.stack([from_left[:, half:], from_right[:, half:]]), n_t)
    partner_left_a = to_right[1]
    partner_right_a = to_left[1]
    partner_far_a = jnp.concatenate(
        [
            shifted(partner_left_a[:, :quarter], step, n_t),
            shifted(partner_right_a[:, quarter:], -step, n_t),
        ],
        axis=1,
    )
    partner_far_b = swapped(far[:, half:], n_t)
    return ready, [
        (t, own),
        (t ^ 1, partner),
        ((t - step) % n_t, from_left),
        ((t + step) % n_t, from_right),
        ((t + 2 * step) % n_t, far),
        ((t - step) % n_t ^ 1, jnp.concatenate([partner_left_a, partner_b[0]], axis=1)),
        ((t + step) % n_t ^ 1, jnp.concatenate([partner_right_a, partner_b[1]], axis=1)),
        ((t + 2 * step) % n_t ^ 1, jnp.concatenate([partner_far_a, partner_far_b], axis=1)),
    ]


def body(perambulators, elementals, src_times, diagrams):
    propagators = perambulators[0]
    own_elemental = elementals[0, 0]
    block_order = propagators.shape[1]
    n_t = lax.axis_size("tsink")
    rows = block_order // n_t
    t = lax.axis_index("tsink")
    step = 2
    origins = [
        t, t ^ 1, (t - step) % n_t, (t + step) % n_t,
        (t + 2 * step) % n_t, (t - step) % n_t ^ 1, (t + step) % n_t ^ 1, (t + 2 * step) % n_t ^ 1,
    ]

    def permuted(group):
        return jnp.concatenate(
            [
                lax.dynamic_slice_in_dim(propagators[source], origin * rows, rows, 1)
                for origin in group
                for source in range(NSRC)
            ],
            axis=1,
        )

    ready = (permuted(origins[:4]), permuted(origins[4:]))
    ready, pieces = source_pieces(own_elemental, src_times, ready)
    def stacked(group, columns):
        blocks = jnp.stack(
            [
                jnp.einsum(
                    "sik,sjk->sij", piece, propagators, preferred_element_type=jnp.float32
                ).astype(jnp.bfloat16)
                for _, piece in group
            ]
        )
        return jnp.dot(
            columns, blocks.reshape(-1, block_order), preferred_element_type=jnp.float32
        )

    summed = stacked(pieces[:4], ready[0]) + stacked(pieces[4:], ready[1])
    meson = summed.astype(jnp.bfloat16)

    n_m = lax.axis_size("mom")
    width = 128
    n_b = block_order // width
    grid = meson.reshape(n_b, width, n_b, width).transpose(0, 2, 1, 3).reshape(n_b * n_b, width, width)
    pairs = [(row, col) for col in range(n_b) for row in range(col + 1)]
    upper = grid[np.array([row * n_b + col for row, col in pairs])]
    upper_t = jnp.swapaxes(grid[np.array([col * n_b + row for row, col in pairs])], 1, 2)
    row_index = lax.broadcasted_iota(jnp.int32, (width, width), 0)
    col_index = lax.broadcasted_iota(jnp.int32, (width, width), 1)
    triangle = jnp.where(row_index < col_index, 1.0, jnp.where(row_index == col_index, 0.5, 0.0))
    on_diagonal = np.array([row == col for row, col in pairs])[:, None, None]
    weight = jnp.where(on_diagonal, triangle[None], 1.0).astype(jnp.bfloat16)
    upper = (upper * weight).reshape(-1, width)
    upper_t = upper_t.reshape(-1, width)
    share = upper.shape[0] // n_m
    slices = jnp.concatenate(
        [upper.reshape(n_m, share, width), upper_t.reshape(n_m, share, width)], axis=1
    )
    received = lax.all_to_all(slices, "mom", 0, 0)
    own_rows = received[:, :share].reshape(n_m, share * width)
    own_cols = received[:, share:].reshape(n_m, share * width)
    partial = lax.dot_general(
        own_rows, own_cols, (((1,), (1,)), ((), ())), preferred_element_type=jnp.float32
    )
    partial = partial + partial.T
    per_diagram = partial[diagrams[:, 0], diagrams[:, 1]]
    spread = lax.all_to_all(per_diagram.reshape(n_m, -1), "mom", 0, 0)
    correlators = (jnp.sum(spread, axis=0) / block_order)[:, None]
    return (meson[None, None], correlators)


def solution(mesh):
    in_specs = (P("tsink", None, None, None), P("tsink", "mom", None, None), P(), P())
    out_specs = (P("tsink", "mom", None, None), P("mom", "tsink"))
    return jax.shard_map(body, mesh=mesh, in_specs=in_specs, out_specs=out_specs, check_vma=False)
```

```python
import numpy as np
import jax
import jax.numpy as jnp
from jax import lax
from jax.sharding import PartitionSpec as P

NSRC = 4


def shifted(block, offset, n_t):
    pairs = [(t, (t + offset) % n_t) for t in range(n_t)]
    return lax.ppermute(block, "tsink", pairs)


def swapped(block, n_t):
    return lax.ppermute(block, "tsink", [(t, t ^ 1) for t in range(n_t)])


def source_pieces(own_elemental, src_times):
    n_t = lax.axis_size("tsink")
    order = own_elemental.shape[0]
    rows = order // n_t
    half = rows // 2
    quarter = half // 2
    pieces = own_elemental.reshape(n_t, rows, order)
    received = lax.all_to_all(pieces, "tsink", 0, 0)
    own = received[src_times]
    t = lax.axis_index("tsink")
    step = 2
    partner = swapped(own, n_t)
    from_left = shifted(own, step, n_t)
    from_right = shifted(own, -step, n_t)
    to_right = shifted(jnp.stack([from_left[:, :half], partner[:, :half]]), step, n_t)
    to_left = shifted(jnp.stack([from_right[:, half:], partner[:, :half]]), -step, n_t)
    far = jnp.concatenate([to_right[0], to_left[0]], axis=1)
    partner_b = swapped(jnp.stack([from_left[:, half:], from_right[:, half:]]), n_t)
    partner_left_a = to_right[1]
    partner_right_a = to_left[1]
    partner_far_a = jnp.concatenate(
        [
            shifted(partner_left_a[:, :quarter], step, n_t),
            shifted(partner_right_a[:, quarter:], -step, n_t),
        ],
        axis=1,
    )
    partner_far_b = swapped(far[:, half:], n_t)
    return [
        (t, own),
        (t ^ 1, partner),
        ((t - step) % n_t, from_left),
        ((t + step) % n_t, from_right),
        ((t + 2 * step) % n_t, far),
        ((t - step) % n_t ^ 1, jnp.concatenate([partner_left_a, partner_b[0]], axis=1)),
        ((t + step) % n_t ^ 1, jnp.concatenate([partner_right_a, partner_b[1]], axis=1)),
        ((t + 2 * step) % n_t ^ 1, jnp.concatenate([partner_far_a, partner_far_b], axis=1)),
    ]


def body(perambulators, elementals, src_times, diagrams):
    propagators = perambulators[0]
    own_elemental = elementals[0, 0]
    block_order = propagators.shape[1]
    pieces = source_pieces(own_elemental, src_times)
    rows = pieces[0][1].shape[1]
    def stacked(group):
        columns = jnp.concatenate(
            [
                lax.dynamic_slice_in_dim(propagators[source], origin * rows, rows, 1)
                for origin, _ in group
                for source in range(NSRC)
            ],
            axis=1,
        )
        blocks = jnp.stack(
            [
                jnp.einsum(
                    "sik,sjk->sij", piece, propagators, preferred_element_type=jnp.float32
                ).astype(jnp.bfloat16)
                for _, piece in group
            ]
        )
        return jnp.dot(
            columns, blocks.reshape(-1, block_order), preferred_element_type=jnp.float32
        )

    summed = stacked(pieces[:4]) + stacked(pieces[4:])
    meson = summed.astype(jnp.bfloat16)

    n_m = lax.axis_size("mom")
    width = 128
    n_b = block_order // width
    grid = meson.reshape(n_b, width, n_b, width).transpose(0, 2, 1, 3).reshape(n_b * n_b, width, width)
    pairs = [(row, col) for col in range(n_b) for row in range(col + 1)]
    upper = grid[np.array([row * n_b + col for row, col in pairs])]
    upper_t = jnp.swapaxes(grid[np.array([col * n_b + row for row, col in pairs])], 1, 2)
    row_index = lax.broadcasted_iota(jnp.int32, (width, width), 0)
    col_index = lax.broadcasted_iota(jnp.int32, (width, width), 1)
    triangle = jnp.where(row_index < col_index, 1.0, jnp.where(row_index == col_index, 0.5, 0.0))
    on_diagonal = np.array([index for index, (row, col) in enumerate(pairs) if row == col])
    upper = upper.at[on_diagonal].multiply(triangle.astype(jnp.bfloat16)[None])
    upper = upper.reshape(-1, width)
    upper_t = upper_t.reshape(-1, width)
    share = upper.shape[0] // n_m
    slices = jnp.concatenate(
        [upper.reshape(n_m, share, width), upper_t.reshape(n_m, share, width)], axis=1
    )
    received = lax.all_to_all(slices, "mom", 0, 0)
    own_rows = received[:, :share].reshape(n_m, share * width)
    own_cols = received[:, share:].reshape(n_m, share * width)
    partial = lax.dot_general(
        own_rows, own_cols, (((1,), (1,)), ((), ())), preferred_element_type=jnp.float32
    )
    partial = partial + partial.T
    per_diagram = partial[diagrams[:, 0], diagrams[:, 1]]
    spread = lax.all_to_all(per_diagram.reshape(n_m, -1), "mom", 0, 0)
    correlators = (jnp.sum(spread, axis=0) / block_order)[:, None]
    return (meson[None, None], correlators)


def solution(mesh):
    in_specs = (P("tsink", None, None, None), P("tsink", "mom", None, None), P(), P())
    out_specs = (P("tsink", "mom", None, None), P("mom", "tsink"))
    return jax.shard_map(body, mesh=mesh, in_specs=in_specs, out_specs=out_specs, check_vma=False)
```

```python
import numpy as np
import jax
import jax.numpy as jnp
from jax import lax
from jax.sharding import PartitionSpec as P

NSRC = 4


def shifted(block, offset, n_t):
    pairs = [(t, (t + offset) % n_t) for t in range(n_t)]
    return lax.ppermute(block, "tsink", pairs)


def swapped(block, n_t):
    return lax.ppermute(block, "tsink", [(t, t ^ 1) for t in range(n_t)])


def source_pieces(own_elemental, src_times):
    n_t = lax.axis_size("tsink")
    order = own_elemental.shape[0]
    rows = order // n_t
    half = rows // 2
    quarter = half // 2
    pieces = own_elemental.reshape(n_t, rows, order)
    received = lax.all_to_all(pieces, "tsink", 0, 0)
    own = received[src_times]
    t = lax.axis_index("tsink")
    step = 2
    partner = swapped(own, n_t)
    from_left = shifted(own, step, n_t)
    from_right = shifted(own, -step, n_t)
    far = jnp.concatenate(
        [shifted(from_left[:, :half], step, n_t), shifted(from_right[:, half:], -step, n_t)], axis=1
    )
    partner_b = swapped(jnp.stack([from_left[:, half:], from_right[:, half:]]), n_t)
    partner_left_a = shifted(partner[:, :half], step, n_t)
    partner_right_a = shifted(partner[:, :half], -step, n_t)
    partner_far_a = jnp.concatenate(
        [
            shifted(partner_left_a[:, :quarter], step, n_t),
            shifted(partner_right_a[:, quarter:], -step, n_t),
        ],
        axis=1,
    )
    partner_far_b = swapped(far[:, half:], n_t)
    return [
        (t, own),
        (t ^ 1, partner),
        ((t - step) % n_t, from_left),
        ((t + step) % n_t, from_right),
        ((t + 2 * step) % n_t, far),
        ((t - step) % n_t ^ 1, jnp.concatenate([partner_left_a, partner_b[0]], axis=1)),
        ((t + step) % n_t ^ 1, jnp.concatenate([partner_right_a, partner_b[1]], axis=1)),
        ((t + 2 * step) % n_t ^ 1, jnp.concatenate([partner_far_a, partner_far_b], axis=1)),
    ]


def body(perambulators, elementals, src_times, diagrams):
    propagators = perambulators[0]
    own_elemental = elementals[0, 0]
    block_order = propagators.shape[1]
    pieces = source_pieces(own_elemental, src_times)
    rows = pieces[0][1].shape[1]
    def stacked(group):
        columns = jnp.concatenate(
            [
                lax.dynamic_slice_in_dim(propagators[source], origin * rows, rows, 1)
                for origin, _ in group
                for source in range(NSRC)
            ],
            axis=1,
        )
        blocks = jnp.stack(
            [
                jnp.einsum(
                    "sik,sjk->sij", piece, propagators, preferred_element_type=jnp.float32
                ).astype(jnp.bfloat16)
                for _, piece in group
            ]
        )
        return jnp.dot(
            columns, blocks.reshape(-1, block_order), preferred_element_type=jnp.float32
        )

    summed = stacked(pieces[:4]) + stacked(pieces[4:])
    meson = summed.astype(jnp.bfloat16)

    n_m = lax.axis_size("mom")
    width = 128
    n_b = block_order // width
    grid = meson.reshape(n_b, width, n_b, width).transpose(0, 2, 1, 3).reshape(n_b * n_b, width, width)
    pairs = [(row, col) for col in range(n_b) for row in range(col + 1)]
    upper = grid[np.array([row * n_b + col for row, col in pairs])]
    upper_t = jnp.swapaxes(grid[np.array([col * n_b + row for row, col in pairs])], 1, 2)
    row_index = lax.broadcasted_iota(jnp.int32, (width, width), 0)
    col_index = lax.broadcasted_iota(jnp.int32, (width, width), 1)
    triangle = jnp.where(row_index < col_index, 1.0, jnp.where(row_index == col_index, 0.5, 0.0))
    on_diagonal = np.array([row == col for row, col in pairs])[:, None, None]
    weight = jnp.where(on_diagonal, triangle[None], 1.0).astype(jnp.bfloat16)
    upper = (upper * weight).reshape(-1, width)
    upper_t = upper_t.reshape(-1, width)
    share = upper.shape[0] // n_m
    slices = jnp.concatenate(
        [upper.reshape(n_m, share, width), upper_t.reshape(n_m, share, width)], axis=1
    )
    received = lax.all_to_all(slices, "mom", 0, 0)
    own_rows = received[:, :share].reshape(n_m, share * width)
    own_cols = received[:, share:].reshape(n_m, share * width)
    partial = lax.dot_general(
        own_rows, own_cols, (((1,), (1,)), ((), ())), preferred_element_type=jnp.float32
    )
    partial = partial + partial.T
    per_diagram = partial[diagrams[:, 0], diagrams[:, 1]]
    spread = lax.all_to_all(per_diagram.reshape(n_m, -1), "mom", 0, 0)
    correlators = (jnp.sum(spread, axis=0) / block_order)[:, None]
    return (meson[None, None], correlators)


def solution(mesh):
    in_specs = (P("tsink", None, None, None), P("tsink", "mom", None, None), P(), P())
    out_specs = (P("tsink", "mom", None, None), P("mom", "tsink"))
    return jax.shard_map(body, mesh=mesh, in_specs=in_specs, out_specs=out_specs, check_vma=False)
```
